32 devices in a mesh: section: 8 (over z, core), seq: 4 (over y, x).
Axes of the slice: x: 2, y: 2, z: 4, core: 2. Of those that a mesh axis runs over, the one named last changes fastest.
Arguments:
- queries: bfloat16 [8, 512, 8192], P('section', 'seq'), may hold values from -48 to 48
- key_states: bfloat16 [8, 512, 1024], P('section', 'seq'), may hold values from -6 to 6
- section_value_states: bfloat16 [8, 512, 1024], P('section', 'seq'), may hold values from -6 to 6
- out_grad: bfloat16 [8, 512, 8192], P('section', 'seq'), may hold values from -1.5 to 1.5
- layer_input: bfloat16 [8, 512, 8192], P('section', 'seq'), may hold values from -6 to 6
- doc_segments: int32 [8, 512], P('section', 'seq'), may hold values from 0 to 3, never falling along the last dimension, each value on 1 to 256 neighbouring positions
Outputs:
- query_grad: bfloat16 [8, 512, 8192], P('section', 'seq')
- key_grad: bfloat16 [8, 512, 1024], P('section', 'seq')
- weight_grad: bfloat16 [8, 8192, 1024], P('section', None, 'seq')
The draws below stay inside these ranges and needn't reach their ends.
Inputs may be any that keep to these rules, and one draw needn't show every extreme that they name: `doc_segments`: document numbers never fall along a section's positions; a document holds at most 256 positions.
All inputs are finite; a program needn't handle non-finite values.
Results may differ from the reference program's by a relative error of at most 0.012.
The reference program's roundings to bfloat16 on the way count: a program that leaves them out, or rounds other values in their place, can miss the bound.
Values may be sent and summed in bfloat16 or wider, within the bound.
No kernel may reach another device: no remote copies, remote signals or barrier semaphores. Data moves between devices by JAX's collectives and lax.ppermute only.
A program may use at most 128 MiB of HBM per device.

```python
import math
import jax
import jax.numpy as jnp
import numpy as np
from jax import lax

D = 8192
QUERY_HEADS = 64
KEY_VALUE_HEADS = 8
HEAD_WIDTH = 128
SECTION_LENGTH = 512
RELAY_SECTIONS = 8


def drawn_pair(key):
    base = jax.random.fold_in(key, 11)
    key_sample, query_draw = jax.random.split(base, 2)
    key_entries = jnp.clip(jax.random.normal(key_sample, (RELAY_SECTIONS, SECTION_LENGTH, KEY_VALUE_HEADS, HEAD_WIDTH), jnp.float32), -6.0, 6.0)
    query_entries = jnp.clip(jax.random.normal(query_draw, (RELAY_SECTIONS, SECTION_LENGTH, QUERY_HEADS, HEAD_WIDTH), jnp.float32), -6.0, 6.0)
    return (query_entries.reshape(RELAY_SECTIONS, SECTION_LENGTH, QUERY_HEADS * HEAD_WIDTH), key_entries.reshape(RELAY_SECTIONS, SECTION_LENGTH, KEY_VALUE_HEADS * HEAD_WIDTH))


def draw_queries(key, part):
    return drawn_pair(key)[0].astype(jnp.bfloat16)


def draw_key_states(key, part):
    return drawn_pair(key)[1].astype(jnp.bfloat16)


def levels(key, dims, cuts, smallest, high):
    def one(axis_at, blocks):
        heights = jax.random.uniform(jax.random.fold_in(jax.random.fold_in(key, 6), axis_at), (blocks,), jnp.float32, smallest / len(cuts), high / len(cuts))
        return jnp.repeat(jnp.exp(heights), dims[axis_at] // blocks).reshape((-1,) + (1,) * (len(dims) - axis_at - 1))

    gain = one(*cuts[0])
    for cut in cuts[1:]:
        gain = gain * one(*cut)
    return gain


def profile(number_of, total, limit, slope):
    portions = [(1 << 20) // math.isqrt(rank ** slope) + 1 for rank in range(2, number_of + 1)]
    surplus, given = total - limit - (number_of - 1), [1] * (number_of - 1)
    while surplus > 0:
        candidates = [i for i in range(number_of - 1) if given[i] < limit]
        whole, left = sum([portions[i] for i in candidates]), surplus
        for i in candidates:
            addition = min(limit - given[i], max(1, left * portions[i] // whole), surplus)
            given[i] = given[i] + addition
            surplus = surplus - addition
    return np.array([limit] + given)


def uneven_parts(key, number_of, total, most, lean):
    if number_of == 2:
        one = jax.random.randint(key, (), max(1, total - most), min(most, total - 1) + 1)
        return jnp.stack([one, total - one])
    sizes = jnp.asarray(profile(number_of, total, most, lean), jnp.int32)
    couples = (number_of - 1) // 2
    donor, taker = sizes[1:1 + 2 * couples:2], sizes[2:2 + 2 * couples:2]
    slack = jnp.minimum(donor - 1, most - taker)
    moved = jax.random.randint(jax.random.fold_in(key, 1), (couples,), 0, 1 << 20) % (slack + 1)
    sizes = sizes.at[1:1 + 2 * couples:2].set(donor - moved).at[2:2 + 2 * couples:2].set(taker + moved)
    return sizes[jax.random.permutation(jax.random.fold_in(key, 2), number_of)]


def noise(own_key, shape, scale, reach, cuts=(), held_as=jnp.bfloat16):
    level = levels(own_key, shape, cuts, -0.22, 0.18) if cuts else 1.0
    values = jax.random.normal(own_key, shape, jnp.float32) * scale * level
    return jnp.minimum(jnp.maximum(values, -reach), reach).astype(held_as)


def setup_inputs(seed: int = 0) -> dict:
    seeds = jax.random.split(jax.random.key(seed), 7)
    queries = draw_queries(jax.random.fold_in(seeds[6], 71), 0)
    key_states = draw_key_states(jax.random.fold_in(seeds[6], 71), 0)
    section_value_states = noise(seeds[2], (RELAY_SECTIONS, SECTION_LENGTH, KEY_VALUE_HEADS * HEAD_WIDTH), 1.0, 6.0, ((0, 8), (1, 4)))
    out_grad = noise(seeds[3], (RELAY_SECTIONS, SECTION_LENGTH, QUERY_HEADS * HEAD_WIDTH), 0.25, 1.5, ((0, 8), (1, 4)))
    layer_input = noise(seeds[4], (RELAY_SECTIONS, SECTION_LENGTH, D), 1.0, 6.0, ((0, 8), (1, 4)))
    doc_segments = jax.vmap(lambda own: jnp.searchsorted(jnp.cumsum(uneven_parts(own, 4, SECTION_LENGTH, SECTION_LENGTH // 2, 2)), jnp.arange(SECTION_LENGTH), side="right"))(jax.random.split(seeds[5], RELAY_SECTIONS)).reshape((RELAY_SECTIONS, SECTION_LENGTH)).astype(jnp.int32)
    return dict(queries=queries, key_states=key_states, section_value_states=section_value_states, out_grad=out_grad, layer_input=layer_input, doc_segments=doc_segments)


def group_pass(query_group, key_col, value_col, grad_group, allowed):
    scale_factor = 1.0 / math.sqrt(key_col.shape[1])

    def one_head(totals, head_inputs):
        query_one, grad_one = head_inputs
        key_acc, value_acc = totals
        scores = jnp.dot(query_one, key_col.T, preferred_element_type=jnp.float32) * scale_factor
        scores = jnp.where(allowed, scores, -jnp.inf)
        row_max = lax.optimization_barrier(jnp.max(scores, axis=1, keepdims=True))
        weights = jnp.exp(scores - row_max)
        attention = weights / lax.optimization_barrier(jnp.sum(weights, axis=1, keepdims=True))
        probs_low = attention.astype(jnp.bfloat16)
        attended = jnp.dot(probs_low, value_col, preferred_element_type=jnp.float32).astype(jnp.bfloat16)
        attended = lax.optimization_barrier(attended)
        row_delta = lax.optimization_barrier(jnp.sum(grad_one.astype(jnp.float32) * attended.astype(jnp.float32), axis=1, keepdims=True))
        dprobs = jnp.dot(grad_one, value_col.T, preferred_element_type=jnp.float32)
        dscores = (attention * (dprobs - row_delta) * scale_factor).astype(jnp.bfloat16)
        query_part = jnp.dot(dscores, key_col, preferred_element_type=jnp.float32).astype(jnp.bfloat16)
        key_acc = key_acc + jnp.dot(dscores.T, query_one, preferred_element_type=jnp.float32)
        value_acc = value_acc + jnp.dot(probs_low.T, grad_one, preferred_element_type=jnp.float32)
        return ((key_acc, value_acc), query_part)
    starting = jnp.zeros(key_col.shape, jnp.float32)
    (key_acc, value_acc), query_parts = lax.scan(one_head, (starting, starting), (query_group, grad_group))
    return (query_parts, key_acc.astype(jnp.bfloat16), value_acc.astype(jnp.bfloat16))

def attention_grads(query_cols, key_cols, value_cols, grad_cols, doc_ids):
    length = query_cols.shape[0]
    kv_heads = key_cols.shape[1] // HEAD_WIDTH
    q_heads = query_cols.shape[1] // HEAD_WIDTH
    group_size = q_heads // kv_heads
    position = jnp.arange(length, dtype=jnp.int32)
    allowed = (position[:, None] >= position[None, :]) & (doc_ids[:, None] == doc_ids[None, :])
    query_split = query_cols.reshape(length, kv_heads, group_size, HEAD_WIDTH).transpose(1, 2, 0, 3)
    grad_split = grad_cols.reshape(length, kv_heads, group_size, HEAD_WIDTH).transpose(1, 2, 0, 3)
    key_split = key_cols.reshape(length, kv_heads, HEAD_WIDTH).transpose(1, 0, 2)
    value_split = value_cols.reshape(length, kv_heads, HEAD_WIDTH).transpose(1, 0, 2)

    def per_group(inputs):
        return group_pass(inputs[0], inputs[1], inputs[2], inputs[3], allowed)
    query_parts, key_parts, value_parts = lax.map(per_group, (query_split, key_split, value_split, grad_split))
    query_out = query_parts.transpose(2, 0, 1, 3).reshape(length, q_heads * HEAD_WIDTH)
    key_out = key_parts.transpose(1, 0, 2).reshape(length, kv_heads * HEAD_WIDTH)
    value_out = value_parts.transpose(1, 0, 2).reshape(length, kv_heads * HEAD_WIDTH)
    return (query_out, key_out, value_out)

def reference(queries, key_states, section_value_states, out_grad, layer_input, doc_segments):

    def per_section(inputs):
        query_cols, key_cols, value_cols, grad_cols, layer_rows, doc_ids = inputs
        query_out, key_out, value_out = attention_grads(query_cols, key_cols, value_cols, grad_cols, doc_ids)
        section_grad = jnp.dot(layer_rows.T, value_out, preferred_element_type=jnp.float32)
        return (query_out, key_out, section_grad)
    query_grad, key_grad, section_grad = lax.map(per_section, (queries, key_states, section_value_states, out_grad, layer_input, doc_segments))
    weight_grad = (section_grad + section_grad[::-1]).astype(jnp.bfloat16)
    return (query_grad, key_grad, weight_grad)
```

```python
import math

import jax
import jax.numpy as jnp
from jax import lax
from jax.sharding import PartitionSpec as P

HEAD_WIDTH = 128


def group_pass(query_group, key_col, value_col, grad_group, allowed):
    scale_factor = 1.0 / math.sqrt(key_col.shape[1])

    def one_head(totals, head_inputs):
        query_one, grad_one = head_inputs
        key_acc, value_acc = totals
        scores = jnp.dot(query_one, key_col.T, preferred_element_type=jnp.float32) * scale_factor
        scores = jnp.where(allowed, scores, -jnp.inf)
        row_max = jnp.max(scores, axis=1, keepdims=True)
        weights = jnp.exp(scores - row_max)
        attention = weights / jnp.sum(weights, axis=1, keepdims=True)
        probs_low = attention.astype(jnp.bfloat16)
        attended = jnp.dot(probs_low, value_col, preferred_element_type=jnp.float32).astype(
            jnp.bfloat16
        )
        attended = lax.optimization_barrier(attended)
        row_delta = jnp.sum(
            grad_one.astype(jnp.float32) * attended.astype(jnp.float32), axis=1, keepdims=True
        )
        dprobs = jnp.dot(grad_one, value_col.T, preferred_element_type=jnp.float32)
        dscores = (attention * (dprobs - row_delta) * scale_factor).astype(jnp.bfloat16)
        query_part = jnp.dot(dscores, key_col, preferred_element_type=jnp.float32).astype(
            jnp.bfloat16
        )
        key_acc = key_acc + jnp.dot(dscores.T, query_one, preferred_element_type=jnp.float32)
        value_acc = value_acc + jnp.dot(probs_low.T, grad_one, preferred_element_type=jnp.float32)
        return ((key_acc, value_acc), query_part)

    starting = jnp.zeros(key_col.shape, jnp.float32)
    (key_acc, value_acc), query_parts = lax.scan(
        one_head, (starting, starting), (query_group, grad_group)
    )
    return (query_parts, key_acc.astype(jnp.bfloat16), value_acc.astype(jnp.bfloat16))


def attention_grads(query_cols, key_cols, value_cols, grad_cols, doc_ids):
    length = query_cols.shape[0]
    kv_heads = key_cols.shape[1] // HEAD_WIDTH
    q_heads = query_cols.shape[1] // HEAD_WIDTH
    group_size = q_heads // kv_heads
    position = jnp.arange(length, dtype=jnp.int32)
    allowed = (position[:, None] >= position[None, :]) & (doc_ids[:, None] == doc_ids[None, :])
    query_split = query_cols.reshape(length, kv_heads, group_size, HEAD_WIDTH).transpose(1, 2, 0, 3)
    grad_split = grad_cols.reshape(length, kv_heads, group_size, HEAD_WIDTH).transpose(1, 2, 0, 3)
    key_split = key_cols.reshape(length, kv_heads, HEAD_WIDTH).transpose(1, 0, 2)
    value_split = value_cols.reshape(length, kv_heads, HEAD_WIDTH).transpose(1, 0, 2)

    def per_group(inputs):
        return group_pass(inputs[0], inputs[1], inputs[2], inputs[3], allowed)

    query_parts, key_parts, value_parts = lax.map(
        per_group, (query_split, key_split, value_split, grad_split)
    )
    query_out = query_parts.transpose(2, 0, 1, 3).reshape(length, q_heads * HEAD_WIDTH)
    key_out = key_parts.transpose(1, 0, 2).reshape(length, kv_heads * HEAD_WIDTH)
    value_out = value_parts.transpose(1, 0, 2).reshape(length, kv_heads * HEAD_WIDTH)
    return (query_out, key_out, value_out)


def row_product(shard_rows, value_rows):
    return lax.dot_general(
        shard_rows, value_rows, (((0,), (0,)), ((), ())), preferred_element_type=jnp.float32
    )


def local(queries, key_states, section_value_states, out_grad, layer_input, doc_segments):
    section_count = lax.axis_size("section")
    mirror = [(i, section_count - 1 - i) for i in range(section_count)]
    mirror_rows = lax.ppermute(layer_input[0], "section", mirror)
    query_head, key_head, value_head, grad_head = (
        lax.all_to_all(queries[0], "seq", split_axis=1, concat_axis=0, tiled=True),
        lax.all_to_all(key_states[0], "seq", split_axis=1, concat_axis=0, tiled=True),
        lax.all_to_all(section_value_states[0], "seq", split_axis=1, concat_axis=0, tiled=True),
        lax.all_to_all(out_grad[0], "seq", split_axis=1, concat_axis=0, tiled=True),
    )
    doc_ids = lax.all_gather(doc_segments[0], "seq", axis=0, tiled=True)
    query_out, key_out, value_out = attention_grads(
        query_head, key_head, value_head, grad_head, doc_ids
    )
    query_back, key_back = (
        lax.all_to_all(query_out, "seq", split_axis=0, concat_axis=1, tiled=True),
        lax.all_to_all(key_out, "seq", split_axis=0, concat_axis=1, tiled=True),
    )
    both_rows = jnp.concatenate([layer_input[0], mirror_rows], axis=0)
    gathered = lax.all_gather(both_rows, "seq", axis=0, tiled=True)
    mirror_value = lax.ppermute(value_out, "section", mirror)
    seq_count = lax.axis_size("seq")
    chunk = value_out.shape[0] // seq_count
    both_values = jnp.stack(
        [value_out.reshape(seq_count, chunk, -1), mirror_value.reshape(seq_count, chunk, -1)],
        axis=1,
    ).reshape(2 * value_out.shape[0], value_out.shape[1])
    paired = row_product(gathered, both_values)
    return (query_back[None], key_back[None], paired.astype(jnp.bfloat16)[None])


def solution(mesh):
    in_specs = (
        P("section", "seq", None),
        P("section", "seq", None),
        P("section", "seq", None),
        P("section", "seq", None),
        P("section", "seq", None),
        P("section", "seq"),
    )
    out_specs = (P("section", "seq", None), P("section", "seq", None), P("section", None, "seq"))
    return jax.shard_map(local, mesh=mesh, in_specs=in_specs, out_specs=out_specs, check_vma=False)
```

```python
import math

import jax
import jax.numpy as jnp
from jax import lax
from jax.experimental import pallas as pl
from jax.experimental.pallas import tpu as pltpu
from jax.sharding import PartitionSpec as P

HEAD_WIDTH = 128


def attention_kernel(query_ref, key_ref, value_ref, grad_ref, doc_col_ref, doc_row_ref,
                     query_out_ref, key_out_ref, value_out_ref):
    head, tile = pl.program_id(1), pl.program_id(2)
    rows, length = query_ref.shape[0], key_ref.shape[0]
    scale_factor = 1.0 / math.sqrt(key_ref.shape[1])

    @pl.when((head == 0) & (tile == 0))
    def _():
        key_out_ref[...] = jnp.zeros(key_out_ref.shape, jnp.float32)
        value_out_ref[...] = jnp.zeros(value_out_ref.shape, jnp.float32)

    query_one, grad_one = query_ref[...], grad_ref[...]
    key_col, value_col = key_ref[...], value_ref[...]
    row_pos = tile * rows + lax.broadcasted_iota(jnp.int32, (rows, length), 0)
    col_pos = lax.broadcasted_iota(jnp.int32, (rows, length), 1)
    allowed = (row_pos >= col_pos) & (doc_col_ref[...] == doc_row_ref[...])
    contract_last = (((1,), (1,)), ((), ()))
    contract_first = (((0,), (0,)), ((), ()))
    scores = lax.dot_general(query_one, key_col, contract_last,
                             preferred_element_type=jnp.float32) * scale_factor
    scores = jnp.where(allowed, scores, -jnp.inf)
    row_max = jnp.max(scores, axis=1, keepdims=True)
    weights = jnp.exp(scores - row_max)
    attention = weights / jnp.sum(weights, axis=1, keepdims=True)
    probs_low = attention.astype(jnp.bfloat16)
    attended = jnp.dot(probs_low, value_col, preferred_element_type=jnp.float32).astype(jnp.bfloat16)
    row_delta = jnp.sum(grad_one.astype(jnp.float32) * attended.astype(jnp.float32),
                        axis=1, keepdims=True)
    dprobs = lax.dot_general(grad_one, value_col, contract_last,
                             preferred_element_type=jnp.float32)
    dscores = (attention * (dprobs - row_delta) * scale_factor).astype(jnp.bfloat16)
    query_out_ref[...] = jnp.dot(dscores, key_col,
                                 preferred_element_type=jnp.float32).astype(jnp.bfloat16)
    key_out_ref[...] += lax.dot_general(dscores, query_one, contract_first,
                                        preferred_element_type=jnp.float32)
    value_out_ref[...] += lax.dot_general(probs_low, grad_one, contract_first,
                                          preferred_element_type=jnp.float32)


def attention_grads(query_cols, key_cols, value_cols, grad_cols, doc_ids):
    length = query_cols.shape[0]
    kv_heads = key_cols.shape[1] // HEAD_WIDTH
    q_heads = query_cols.shape[1] // HEAD_WIDTH
    group_size = q_heads // kv_heads
    rows = min(length, 256)
    tiles = length // rows
    head_block = lambda g, h, t: (t, g * group_size + h)
    kv_block = lambda g, h, t: (0, g)
    query_out, key_acc, value_acc = pl.pallas_call(
        attention_kernel,
        grid=(kv_heads, group_size, tiles),
        in_specs=[
            pl.BlockSpec((rows, HEAD_WIDTH), head_block),
            pl.BlockSpec((length, HEAD_WIDTH), kv_block),
            pl.BlockSpec((length, HEAD_WIDTH), kv_block),
            pl.BlockSpec((rows, HEAD_WIDTH), head_block),
            pl.BlockSpec((rows, 1), lambda g, h, t: (t, 0)),
            pl.BlockSpec((1, length), lambda g, h, t: (0, 0)),
        ],
        out_specs=[
            pl.BlockSpec((rows, HEAD_WIDTH), head_block),
            pl.BlockSpec((length, HEAD_WIDTH), kv_block),
            pl.BlockSpec((length, HEAD_WIDTH), kv_block),
        ],
        out_shape=[
            jax.ShapeDtypeStruct(query_cols.shape, jnp.bfloat16),
            jax.ShapeDtypeStruct(key_cols.shape, jnp.float32),
            jax.ShapeDtypeStruct(value_cols.shape, jnp.float32),
        ],
        compiler_params=pltpu.CompilerParams(
            dimension_semantics=("arbitrary", "arbitrary", "arbitrary"),
            vmem_limit_bytes=48 * 1024 * 1024,
        ),
    )(query_cols, key_cols, value_cols, grad_cols, doc_ids.reshape(length, 1),
      doc_ids.reshape(1, length))
    return (query_out, key_acc.astype(jnp.bfloat16), value_acc.astype(jnp.bfloat16))


def row_product(shard_rows, value_rows):
    return lax.dot_general(
        shard_rows, value_rows, (((0,), (0,)), ((), ())), preferred_element_type=jnp.float32
    )


def local(queries, key_states, section_value_states, out_grad, layer_input, doc_segments):
    section_count = lax.axis_size("section")
    mirror = [(i, section_count - 1 - i) for i in range(section_count)]
    mirror_rows = lax.ppermute(layer_input[0], "section", mirror)
    query_head, key_head, value_head, grad_head = (
        lax.all_to_all(queries[0], "seq", split_axis=1, concat_axis=0, tiled=True),
        lax.all_to_all(key_states[0], "seq", split_axis=1, concat_axis=0, tiled=True),
        lax.all_to_all(section_value_states[0], "seq", split_axis=1, concat_axis=0, tiled=True),
        lax.all_to_all(out_grad[0], "seq", split_axis=1, concat_axis=0, tiled=True),
    )
    doc_ids = lax.all_gather(doc_segments[0], "seq", axis=0, tiled=True)
    query_out, key_out, value_out = attention_grads(
        query_head, key_head, value_head, grad_head, doc_ids
    )
    query_back, key_back = (
        lax.all_to_all(query_out, "seq", split_axis=0, concat_axis=1, tiled=True),
        lax.all_to_all(key_out, "seq", split_axis=0, concat_axis=1, tiled=True),
    )
    both_rows = jnp.concatenate([layer_input[0], mirror_rows], axis=0)
    gathered = lax.all_gather(both_rows, "seq", axis=0, tiled=True)
    mirror_value = lax.ppermute(value_out, "section", mirror)
    seq_count = lax.axis_size("seq")
    chunk = value_out.shape[0] // seq_count
    both_values = jnp.stack(
        [value_out.reshape(seq_count, chunk, -1), mirror_value.reshape(seq_count, chunk, -1)],
        axis=1,
    ).reshape(2 * value_out.shape[0], value_out.shape[1])
    paired = row_product(gathered, both_values)
    return (query_back[None], key_back[None], paired.astype(jnp.bfloat16)[None])


def solution(mesh):
    in_specs = (
        P("section", "seq", None),
        P("section", "seq", None),
        P("section", "seq", None),
        P("section", "seq", None),
        P("section", "seq", None),
        P("section", "seq"),
    )
    out_specs = (P("section", "seq", None), P("section", "seq", None), P("section", None, "seq"))
    return jax.shard_map(local, mesh=mesh, in_specs=in_specs, out_specs=out_specs, check_vma=False)
```

```python
import math

import jax
import jax.numpy as jnp
from jax import lax
from jax.experimental import pallas as pl
from jax.experimental.pallas import tpu as pltpu
from jax.sharding import PartitionSpec as P

HEAD_WIDTH = 128


def attention_kernel(query_ref, key_ref, value_ref, grad_ref, doc_col_ref, doc_row_ref,
                     query_out_ref, key_out_ref, value_out_ref):
    head, tile = pl.program_id(1), pl.program_id(2)
    rows, length = query_ref.shape[0], key_ref.shape[0]
    scale_factor = 1.0 / math.sqrt(key_ref.shape[1])

    @pl.when((head == 0) & (tile == 0))
    def _():
        key_out_ref[...] = jnp.zeros(key_out_ref.shape, jnp.float32)
        value_out_ref[...] = jnp.zeros(value_out_ref.shape, jnp.float32)

    query_one, grad_one = query_ref[...], grad_ref[...]
    key_col, value_col = key_ref[...], value_ref[...]
    row_pos = tile * rows + lax.broadcasted_iota(jnp.int32, (rows, length), 0)
    col_pos = lax.broadcasted_iota(jnp.int32, (rows, length), 1)
    allowed = (row_pos >= col_pos) & (doc_col_ref[...] == doc_row_ref[...])
    contract_last = (((1,), (1,)), ((), ()))
    contract_first = (((0,), (0,)), ((), ()))
    scores = lax.dot_general(query_one, key_col, contract_last,
                             preferred_element_type=jnp.float32) * scale_factor
    scores = jnp.where(allowed, scores, -jnp.inf)
    row_max = jnp.max(scores, axis=1, keepdims=True)
    weights = jnp.exp(scores - row_max)
    attention = weights / jnp.sum(weights, axis=1, keepdims=True)
    probs_low = attention.astype(jnp.bfloat16)
    attended = jnp.dot(probs_low, value_col, preferred_element_type=jnp.float32).astype(jnp.bfloat16)
    row_delta = jnp.sum(grad_one.astype(jnp.float32) * attended.astype(jnp.float32),
                        axis=1, keepdims=True)
    dprobs = lax.dot_general(grad_one, value_col, contract_last,
                             preferred_element_type=jnp.float32)
    dscores = (attention * (dprobs - row_delta) * scale_factor).astype(jnp.bfloat16)
    query_out_ref[...] = jnp.dot(dscores, key_col,
                                 preferred_element_type=jnp.float32).astype(jnp.bfloat16)
    key_out_ref[...] += lax.dot_general(dscores, query_one, contract_first,
                                        preferred_element_type=jnp.float32)
    value_out_ref[...] += lax.dot_general(probs_low, grad_one, contract_first,
                                          preferred_element_type=jnp.float32)


def attention_grads(merged, doc_ids, q_width, k_width):
    length = merged.shape[0]
    kv_heads = k_width // HEAD_WIDTH
    group_size = q_width // k_width
    rows = min(length, 256)
    tiles = length // rows
    q_blocks, k_blocks = q_width // HEAD_WIDTH, k_width // HEAD_WIDTH

    def head_at(base):
        return pl.BlockSpec((rows, HEAD_WIDTH), lambda g, h, t: (t, base + g * group_size + h))

    def kv_at(base):
        return pl.BlockSpec((length, HEAD_WIDTH), lambda g, h, t: (0, base + g))

    query_out, key_acc, value_acc = pl.pallas_call(
        attention_kernel,
        grid=(kv_heads, group_size, tiles),
        in_specs=[
            head_at(0),
            kv_at(2 * q_blocks),
            kv_at(2 * q_blocks + k_blocks),
            head_at(q_blocks),
            pl.BlockSpec((rows, 1), lambda g, h, t: (t, 0)),
            pl.BlockSpec((1, length), lambda g, h, t: (0, 0)),
        ],
        out_specs=[
            pl.BlockSpec((rows, HEAD_WIDTH), lambda g, h, t: (t, g * group_size + h)),
            kv_at(0),
            kv_at(0),
        ],
        out_shape=[
            jax.ShapeDtypeStruct((length, q_width), jnp.bfloat16),
            jax.ShapeDtypeStruct((length, k_width), jnp.float32),
            jax.ShapeDtypeStruct((length, k_width), jnp.float32),
        ],
        compiler_params=pltpu.CompilerParams(
            dimension_semantics=("arbitrary", "arbitrary", "arbitrary"),
            vmem_limit_bytes=48 * 1024 * 1024,
        ),
    )(merged, merged, merged, merged, doc_ids.reshape(length, 1), doc_ids.reshape(1, length))
    return (query_out, key_acc.astype(jnp.bfloat16), value_acc.astype(jnp.bfloat16))


def row_product(shard_rows, value_rows):
    return lax.dot_general(
        shard_rows, value_rows, (((0,), (0,)), ((), ())), preferred_element_type=jnp.float32
    )


def local(queries, key_states, section_value_states, out_grad, layer_input, doc_segments):
    section_count = lax.axis_size("section")
    seq_count = lax.axis_size("seq")
    mirror = [(i, section_count - 1 - i) for i in range(section_count)]
    own_rows = layer_input[0]
    own_gathered = lax.all_gather(own_rows, "seq", axis=0, tiled=True)
    mirror_rows = lax.ppermute(own_rows, "section", mirror)
    mirror_gathered = lax.all_gather(mirror_rows, "seq", axis=0, tiled=True)
    positions = queries.shape[1]
    q_width = queries.shape[2] // seq_count
    k_width = key_states.shape[2] // seq_count
    parts = [
        queries[0].reshape(positions, seq_count, q_width),
        out_grad[0].reshape(positions, seq_count, q_width),
        key_states[0].reshape(positions, seq_count, k_width),
        section_value_states[0].reshape(positions, seq_count, k_width),
    ]
    merged = lax.all_to_all(
        jnp.concatenate(parts, axis=2), "seq", split_axis=1, concat_axis=0, tiled=True
    ).reshape(positions * seq_count, 2 * q_width + 2 * k_width)
    doc_ids = lax.all_to_all(
        jnp.broadcast_to(doc_segments, (seq_count, positions)), "seq",
        split_axis=0, concat_axis=0, tiled=True,
    ).reshape(seq_count * positions)
    query_out, key_out, value_out = attention_grads(merged, doc_ids, q_width, k_width)
    query_back, key_back = (
        lax.all_to_all(query_out, "seq", split_axis=0, concat_axis=1, tiled=True),
        lax.all_to_all(key_out, "seq", split_axis=0, concat_axis=1, tiled=True),
    )
    mirror_value = lax.ppermute(value_out, "section", mirror)
    paired = row_product(own_gathered, value_out) + row_product(mirror_gathered, mirror_value)
    return (query_back[None], key_back[None], paired.astype(jnp.bfloat16)[None])


def solution(mesh):
    in_specs = (
        P("section", "seq", None),
        P("section", "seq", None),
        P("section", "seq", None),
        P("section", "seq", None),
        P("section", "seq", None),
        P("section", "seq"),
    )
    out_specs = (P("section", "seq", None), P("section", "seq", None), P("section", None, "seq"))
    return jax.shard_map(local, mesh=mesh, in_specs=in_specs, out_specs=out_specs, check_vma=False)
```

```python
import math

import jax
import jax.numpy as jnp
from jax import lax
from jax.experimental import pallas as pl
from jax.experimental.pallas import tpu as pltpu
from jax.sharding import PartitionSpec as P

HEAD_WIDTH = 128


def attention_kernel(query_ref, key_ref, value_ref, grad_ref, doc_col_ref, doc_row_ref,
                     query_out_ref, key_out_ref, value_out_ref):
    head, tile = pl.program_id(1), pl.program_id(2)
    rows, length = query_ref.shape[0], key_ref.shape[0]
    scale_factor = 1.0 / math.sqrt(key_ref.shape[1])

    @pl.when((head == 0) & (tile == 0))
    def _():
        key_out_ref[...] = jnp.zeros(key_out_ref.shape, jnp.float32)
        value_out_ref[...] = jnp.zeros(value_out_ref.shape, jnp.float32)

    query_one, grad_one = query_ref[...], grad_ref[...]
    key_col, value_col = key_ref[...], value_ref[...]
    row_pos = tile * rows + lax.broadcasted_iota(jnp.int32, (rows, length), 0)
    col_pos = lax.broadcasted_iota(jnp.int32, (rows, length), 1)
    allowed = (row_pos >= col_pos) & (doc_col_ref[...] == doc_row_ref[...])
    contract_last = (((1,), (1,)), ((), ()))
    contract_first = (((0,), (0,)), ((), ()))
    scores = lax.dot_general(query_one, key_col, contract_last,
                             preferred_element_type=jnp.float32) * scale_factor
    scores = jnp.where(allowed, scores, -jnp.inf)
    row_max = jnp.max(scores, axis=1, keepdims=True)
    weights = jnp.exp(scores - row_max)
    attention = weights / jnp.sum(weights, axis=1, keepdims=True)
    probs_low = attention.astype(jnp.bfloat16)
    attended = jnp.dot(probs_low, value_col, preferred_element_type=jnp.float32).astype(jnp.bfloat16)
    row_delta = jnp.sum(grad_one.astype(jnp.float32) * attended.astype(jnp.float32),
                        axis=1, keepdims=True)
    dprobs = lax.dot_general(grad_one, value_col, contract_last,
                             preferred_element_type=jnp.float32)
    dscores = (attention * (dprobs - row_delta) * scale_factor).astype(jnp.bfloat16)
    query_out_ref[...] = jnp.dot(dscores, key_col,
                                 preferred_element_type=jnp.float32).astype(jnp.bfloat16)
    key_out_ref[...] += lax.dot_general(dscores, query_one, contract_first,
                                        preferred_element_type=jnp.float32)
    value_out_ref[...] += lax.dot_general(probs_low, grad_one, contract_first,
                                          preferred_element_type=jnp.float32)


def attention_grads(merged, doc_ids, q_width, k_width):
    length = merged.shape[0]
    kv_heads = k_width // HEAD_WIDTH
    group_size = q_width // k_width
    rows = min(length, 256)
    tiles = length // rows
    q_blocks, k_blocks = q_width // HEAD_WIDTH, k_width // HEAD_WIDTH

    def head_at(base):
        return pl.BlockSpec((rows, HEAD_WIDTH), lambda g, h, t: (t, base + g * group_size + h))

    def kv_at(base):
        return pl.BlockSpec((length, HEAD_WIDTH), lambda g, h, t: (0, base + g))

    query_out, key_acc, value_acc = pl.pallas_call(
        attention_kernel,
        grid=(kv_heads, group_size, tiles),
        in_specs=[
            head_at(0),
            kv_at(2 * q_blocks),
            kv_at(2 * q_blocks + k_blocks),
            head_at(q_blocks),
            pl.BlockSpec((rows, 1), lambda g, h, t: (t, 0)),
            pl.BlockSpec((1, length), lambda g, h, t: (0, 0)),
        ],
        out_specs=[
            pl.BlockSpec((rows, HEAD_WIDTH), lambda g, h, t: (t, g * group_size + h)),
            kv_at(0),
            kv_at(0),
        ],
        out_shape=[
            jax.ShapeDtypeStruct((length, q_width), jnp.bfloat16),
            jax.ShapeDtypeStruct((length, k_width), jnp.float32),
            jax.ShapeDtypeStruct((length, k_width), jnp.float32),
        ],
        compiler_params=pltpu.CompilerParams(
            dimension_semantics=("arbitrary", "arbitrary", "arbitrary"),
            vmem_limit_bytes=48 * 1024 * 1024,
        ),
    )(merged, merged, merged, merged, doc_ids.reshape(length, 1), doc_ids.reshape(1, length))
    return (query_out, key_acc.astype(jnp.bfloat16), value_acc.astype(jnp.bfloat16))


def weight_kernel(*refs):
    value_ref, out_ref = refs[-2], refs[-1]
    contract_first = (((0,), (0,)), ((), ()))
    total = None
    for slot, rows_ref in enumerate(refs[:-2]):
        part = lax.dot_general(rows_ref[...], value_ref[slot], contract_first,
                               preferred_element_type=jnp.float32)
        total = part if total is None else total + part
    out_ref[...] = total.astype(out_ref.dtype)


def weight_grads(row_pieces, value_slots):
    chunk, width = row_pieces[0].shape
    cols = value_slots.shape[2]
    tile = min(width, 512)
    return pl.pallas_call(
        weight_kernel,
        grid=(width // tile,),
        in_specs=[pl.BlockSpec((chunk, tile), lambda i: (0, i)) for _ in row_pieces]
        + [pl.BlockSpec(value_slots.shape, lambda i: (0, 0, 0))],
        out_specs=pl.BlockSpec((tile, cols), lambda i: (i, 0)),
        out_shape=jax.ShapeDtypeStruct((width, cols), jnp.bfloat16),
        compiler_params=pltpu.CompilerParams(dimension_semantics=("arbitrary",)),
    )(*row_pieces, value_slots)


def seq_partner(index, shift, count):
    if count & (count - 1) == 0:
        return index ^ shift
    return (index + shift) % count


def seq_spread(rows, count):
    pieces = [rows]
    for shift in range(1, count):
        pairs = [(seq_partner(i, shift, count), i) for i in range(count)]
        pieces.append(lax.ppermute(rows, "seq", pairs))
    return pieces


def value_slots_of(values, count, index):
    chunk = values.shape[0] // count
    return [
        lax.dynamic_slice_in_dim(values, seq_partner(index, shift, count) * chunk, chunk)
        for shift in range(count)
    ]


def local(queries, key_states, section_value_states, out_grad, layer_input, doc_segments):
    section_count = lax.axis_size("section")
    seq_count = lax.axis_size("seq")
    seq_index = lax.axis_index("seq")
    mirror = [(i, section_count - 1 - i) for i in range(section_count)]
    own_rows = layer_input[0]
    mirror_rows = lax.ppermute(own_rows, "section", mirror)
    positions = queries.shape[1]
    q_width = queries.shape[2] // seq_count
    k_width = key_states.shape[2] // seq_count
    parts = [
        queries[0].reshape(positions, seq_count, q_width),
        out_grad[0].reshape(positions, seq_count, q_width),
        key_states[0].reshape(positions, seq_count, k_width),
        section_value_states[0].reshape(positions, seq_count, k_width),
    ]
    merged = lax.all_to_all(
        jnp.concatenate(parts, axis=2), "seq", split_axis=1, concat_axis=0, tiled=True
    ).reshape(positions * seq_count, 2 * q_width + 2 * k_width)
    doc_ids = lax.all_to_all(
        jnp.broadcast_to(doc_segments, (seq_count, positions)), "seq",
        split_axis=0, concat_axis=0, tiled=True,
    ).reshape(seq_count * positions)
    merged, own_rows = lax.optimization_barrier((merged, own_rows))
    own_pieces = seq_spread(own_rows, seq_count)
    query_out, key_out, value_out = attention_grads(merged, doc_ids, q_width, k_width)
    query_out, key_out, value_out, mirror_rows = lax.optimization_barrier(
        (query_out, key_out, value_out, mirror_rows)
    )
    mirror_pieces = seq_spread(mirror_rows, seq_count)
    query_back, key_back = (
        lax.all_to_all(query_out, "seq", split_axis=0, concat_axis=1, tiled=True),
        lax.all_to_all(key_out, "seq", split_axis=0, concat_axis=1, tiled=True),
    )
    mirror_value = lax.ppermute(value_out, "section", mirror)
    value_slots = jnp.stack(
        value_slots_of(value_out, seq_count, seq_index)
        + value_slots_of(mirror_value, seq_count, seq_index)
    )
    paired = weight_grads(own_pieces + mirror_pieces, value_slots)
    return (query_back[None], key_back[None], paired[None])


def solution(mesh):
    in_specs = (
        P("section", "seq", None),
        P("section", "seq", None),
        P("section", "seq", None),
        P("section", "seq", None),
        P("section", "seq", None),
        P("section", "seq"),
    )
    out_specs = (P("section", "seq", None), P("section", "seq", None), P("section", None, "seq"))
    return jax.shard_map(local, mesh=mesh, in_specs=in_specs, out_specs=out_specs, check_vma=False)
```

```python
import math

import jax
import jax.numpy as jnp
from jax import lax
from jax.experimental import pallas as pl
from jax.experimental.pallas import tpu as pltpu
from jax.sharding import PartitionSpec as P

HEAD_WIDTH = 128


def attention_kernel(query_ref, key_ref, value_ref, grad_ref, doc_col_ref, doc_row_ref,
                     query_out_ref, key_out_ref, value_out_ref):
    head, tile = pl.program_id(1), pl.program_id(2)
    rows, length = query_ref.shape[0], key_ref.shape[0]
    scale_factor = 1.0 / math.sqrt(key_ref.shape[1])

    @pl.when((head == 0) & (tile == 0))
    def _():
        key_out_ref[...] = jnp.zeros(key_out_ref.shape, jnp.float32)
        value_out_ref[...] = jnp.zeros(value_out_ref.shape, jnp.float32)

    query_one, grad_one = query_ref[...], grad_ref[...]
    key_col, value_col = key_ref[...], value_ref[...]
    row_pos = tile * rows + lax.broadcasted_iota(jnp.int32, (rows, length), 0)
    col_pos = lax.broadcasted_iota(jnp.int32, (rows, length), 1)
    allowed = (row_pos >= col_pos) & (doc_col_ref[...] == doc_row_ref[...])
    contract_last = (((1,), (1,)), ((), ()))
    contract_first = (((0,), (0,)), ((), ()))
    scores = lax.dot_general(query_one, key_col, contract_last,
                             preferred_element_type=jnp.float32) * scale_factor
    scores = jnp.where(allowed, scores, -jnp.inf)
    row_max = jnp.max(scores, axis=1, keepdims=True)
    weights = jnp.exp(scores - row_max)
    attention = weights / jnp.sum(weights, axis=1, keepdims=True)
    probs_low = attention.astype(jnp.bfloat16)
    attended = jnp.dot(probs_low, value_col, preferred_element_type=jnp.float32).astype(jnp.bfloat16)
    row_delta = jnp.sum(grad_one.astype(jnp.float32) * attended.astype(jnp.float32),
                        axis=1, keepdims=True)
    dprobs = lax.dot_general(grad_one, value_col, contract_last,
                             preferred_element_type=jnp.float32)
    dscores = (attention * (dprobs - row_delta) * scale_factor).astype(jnp.bfloat16)
    query_out_ref[...] = jnp.dot(dscores, key_col,
                                 preferred_element_type=jnp.float32).astype(jnp.bfloat16)
    key_out_ref[...] += lax.dot_general(dscores, query_one, contract_first,
                                        preferred_element_type=jnp.float32)
    value_out_ref[...] += lax.dot_general(probs_low, grad_one, contract_first,
                                          preferred_element_type=jnp.float32)


def attention_grads(merged, doc_ids, q_width, k_width):
    length = merged.shape[0]
    kv_heads = k_width // HEAD_WIDTH
    group_size = q_width // k_width
    rows = min(length, 256)
    tiles = length // rows
    q_blocks, k_blocks = q_width // HEAD_WIDTH, k_width // HEAD_WIDTH

    def head_at(base):
        return pl.BlockSpec((rows, HEAD_WIDTH), lambda g, h, t: (t, base + g * group_size + h))

    def kv_at(base):
        return pl.BlockSpec((length, HEAD_WIDTH), lambda g, h, t: (0, base + g))

    query_out, key_acc, value_acc = pl.pallas_call(
        attention_kernel,
        grid=(kv_heads, group_size, tiles),
        in_specs=[
            head_at(0),
            kv_at(2 * q_blocks),
            kv_at(2 * q_blocks + k_blocks),
            head_at(q_blocks),
            pl.BlockSpec((rows, 1), lambda g, h, t: (t, 0)),
            pl.BlockSpec((1, length), lambda g, h, t: (0, 0)),
        ],
        out_specs=[
            pl.BlockSpec((rows, HEAD_WIDTH), lambda g, h, t: (t, g * group_size + h)),
            kv_at(0),
            kv_at(0),
        ],
        out_shape=[
            jax.ShapeDtypeStruct((length, q_width), jnp.bfloat16),
            jax.ShapeDtypeStruct((length, k_width), jnp.float32),
            jax.ShapeDtypeStruct((length, k_width), jnp.float32),
        ],
        compiler_params=pltpu.CompilerParams(
            dimension_semantics=("arbitrary", "arbitrary", "arbitrary"),
            vmem_limit_bytes=48 * 1024 * 1024,
        ),
    )(merged, merged, merged, merged, doc_ids.reshape(length, 1), doc_ids.reshape(1, length))
    return (query_out, key_acc.astype(jnp.bfloat16), value_acc.astype(jnp.bfloat16))


def weight_kernel(*refs):
    value_ref, out_ref = refs[-2], refs[-1]
    contract_first = (((0,), (0,)), ((), ()))
    total = None
    for slot, rows_ref in enumerate(refs[:-2]):
        part = lax.dot_general(rows_ref[...], value_ref[slot], contract_first,
                               preferred_element_type=jnp.float32)
        total = part if total is None else total + part
    out_ref[...] = total.astype(out_ref.dtype)


def weight_grads(row_pieces, value_slots):
    chunk, width = row_pieces[0].shape
    cols = value_slots.shape[2]
    tile = min(width, 512)
    return pl.pallas_call(
        weight_kernel,
        grid=(width // tile,),
        in_specs=[pl.BlockSpec((chunk, tile), lambda i: (0, i)) for _ in row_pieces]
        + [pl.BlockSpec(value_slots.shape, lambda i: (0, 0, 0))],
        out_specs=pl.BlockSpec((tile, cols), lambda i: (i, 0)),
        out_shape=jax.ShapeDtypeStruct((width, cols), jnp.bfloat16),
        compiler_params=pltpu.CompilerParams(dimension_semantics=("arbitrary",)),
    )(*row_pieces, value_slots)


def seq_partner(index, shift, count):
    if count & (count - 1) == 0:
        return index ^ shift
    return (index + shift) % count


def seq_spread(rows, count):
    pieces = [rows]
    for shift in range(1, count):
        pairs = [(seq_partner(i, shift, count), i) for i in range(count)]
        pieces.append(lax.ppermute(rows, "seq", pairs))
    return pieces


def value_slots_of(values, count, index):
    chunk = values.shape[0] // count
    return [
        lax.dynamic_slice_in_dim(values, seq_partner(index, shift, count) * chunk, chunk)
        for shift in range(count)
    ]


def local(queries, key_states, section_value_states, out_grad, layer_input, doc_segments):
    section_count = lax.axis_size("section")
    seq_count = lax.axis_size("seq")
    seq_index = lax.axis_index("seq")
    mirror = [(i, section_count - 1 - i) for i in range(section_count)]
    own_rows = layer_input[0]
    mirror_rows = lax.ppermute(own_rows, "section", mirror)
    positions = queries.shape[1]
    q_width = queries.shape[2] // seq_count
    k_width = key_states.shape[2] // seq_count
    parts = [
        queries[0].reshape(positions, seq_count, q_width),
        out_grad[0].reshape(positions, seq_count, q_width),
        key_states[0].reshape(positions, seq_count, k_width),
        section_value_states[0].reshape(positions, seq_count, k_width),
    ]
    merged = lax.all_to_all(
        jnp.concatenate(parts, axis=2), "seq", split_axis=1, concat_axis=0, tiled=True
    ).reshape(positions * seq_count, 2 * q_width + 2 * k_width)
    doc_ids = lax.all_to_all(
        jnp.broadcast_to(doc_segments, (seq_count, positions)), "seq",
        split_axis=0, concat_axis=0, tiled=True,
    ).reshape(seq_count * positions)
    merged, own_rows = lax.optimization_barrier((merged, own_rows))
    own_pieces = seq_spread(own_rows, seq_count)
    query_out, key_out, value_out = attention_grads(merged, doc_ids, q_width, k_width)
    query_out, key_out, value_out, mirror_rows = lax.optimization_barrier(
        (query_out, key_out, value_out, mirror_rows)
    )
    mirror_pieces = seq_spread(mirror_rows, seq_count)
    back = lax.all_to_all(
        jnp.concatenate([query_out, key_out], axis=1), "seq", split_axis=0, concat_axis=0,
        tiled=True,
    ).reshape(seq_count, positions, q_width + k_width)
    query_back = jnp.concatenate([back[j, :, :q_width] for j in range(seq_count)], axis=1)
    key_back = jnp.concatenate([back[j, :, q_width:] for j in range(seq_count)], axis=1)
    mirror_value = lax.ppermute(value_out, "section", mirror)
    value_slots = jnp.stack(
        value_slots_of(value_out, seq_count, seq_index)
        + value_slots_of(mirror_value, seq_count, seq_index)
    )
    paired = weight_grads(own_pieces + mirror_pieces, value_slots)
    return (query_back[None], key_back[None], paired[None])


def solution(mesh):
    in_specs = (
        P("section", "seq", None),
        P("section", "seq", None),
        P("section", "seq", None),
        P("section", "seq", None),
        P("section", "seq", None),
        P("section", "seq"),
    )
    out_specs = (P("section", "seq", None), P("section", "seq", None), P("section", None, "seq"))
    return jax.shard_map(local, mesh=mesh, in_specs=in_specs, out_specs=out_specs, check_vma=False)
```

```python
import math

import jax
import jax.numpy as jnp
from jax import lax
from jax.experimental import pallas as pl
from jax.experimental.pallas import tpu as pltpu
from jax.sharding import PartitionSpec as P

HEAD_WIDTH = 128


def attention_kernel(query_ref, key_ref, value_ref, grad_ref, doc_col_ref, doc_row_ref,
                     query_out_ref, key_out_ref, value_out_ref):
    head, tile = pl.program_id(1), pl.program_id(2)
    rows, length = query_ref.shape[0], key_ref.shape[0]
    scale_factor = 1.0 / math.sqrt(key_ref.shape[1])

    @pl.when((head == 0) & (tile == 0))
    def _():
        key_out_ref[...] = jnp.zeros(key_out_ref.shape, jnp.float32)
        value_out_ref[...] = jnp.zeros(value_out_ref.shape, jnp.float32)

    query_one, grad_one = query_ref[...], grad_ref[...]
    key_col, value_col = key_ref[...], value_ref[...]
    row_pos = tile * rows + lax.broadcasted_iota(jnp.int32, (rows, length), 0)
    col_pos = lax.broadcasted_iota(jnp.int32, (rows, length), 1)
    allowed = (row_pos >= col_pos) & (doc_col_ref[...] == doc_row_ref[...])
    contract_last = (((1,), (1,)), ((), ()))
    contract_first = (((0,), (0,)), ((), ()))
    scores = lax.dot_general(query_one, key_col, contract_last,
                             preferred_element_type=jnp.float32) * scale_factor
    scores = jnp.where(allowed, scores, -jnp.inf)
    row_max = jnp.max(scores, axis=1, keepdims=True)
    weights = jnp.exp(scores - row_max)
    attention = weights / jnp.sum(weights, axis=1, keepdims=True)
    probs_low = attention.astype(jnp.bfloat16)
    attended = jnp.dot(probs_low, value_col, preferred_element_type=jnp.float32).astype(jnp.bfloat16)
    row_delta = jnp.sum(grad_one.astype(jnp.float32) * attended.astype(jnp.float32),
                        axis=1, keepdims=True)
    dprobs = lax.dot_general(grad_one, value_col, contract_last,
                             preferred_element_type=jnp.float32)
    dscores = (attention * (dprobs - row_delta) * scale_factor).astype(jnp.bfloat16)
    query_out_ref[...] = jnp.dot(dscores, key_col,
                                 preferred_element_type=jnp.float32).astype(jnp.bfloat16)
    key_out_ref[...] += lax.dot_general(dscores, query_one, contract_first,
                                        preferred_element_type=jnp.float32)
    value_out_ref[...] += lax.dot_general(probs_low, grad_one, contract_first,
                                          preferred_element_type=jnp.float32)


def attention_grads(merged, doc_ids, q_width, k_width):
    length = merged.shape[0]
    kv_heads = k_width // HEAD_WIDTH
    group_size = q_width // k_width
    rows = min(length, 256)
    tiles = length // rows
    q_blocks, k_blocks = q_width // HEAD_WIDTH, k_width // HEAD_WIDTH

    def head_at(base):
        return pl.BlockSpec((rows, HEAD_WIDTH), lambda g, h, t: (t, base + g * group_size + h))

    def kv_at(base):
        return pl.BlockSpec((length, HEAD_WIDTH), lambda g, h, t: (0, base + g))

    query_out, key_acc, value_acc = pl.pallas_call(
        attention_kernel,
        grid=(kv_heads, group_size, tiles),
        in_specs=[
            head_at(0),
            kv_at(2 * q_blocks),
            kv_at(2 * q_blocks + k_blocks),
            head_at(q_blocks),
            pl.BlockSpec((rows, 1), lambda g, h, t: (t, 0)),
            pl.BlockSpec((1, length), lambda g, h, t: (0, 0)),
        ],
        out_specs=[
            pl.BlockSpec((rows, HEAD_WIDTH), lambda g, h, t: (t, g * group_size + h)),
            kv_at(0),
            kv_at(0),
        ],
        out_shape=[
            jax.ShapeDtypeStruct((length, q_width), jnp.bfloat16),
            jax.ShapeDtypeStruct((length, k_width), jnp.float32),
            jax.ShapeDtypeStruct((length, k_width), jnp.float32),
        ],
        compiler_params=pltpu.CompilerParams(
            dimension_semantics=("arbitrary", "arbitrary", "arbitrary"),
            vmem_limit_bytes=48 * 1024 * 1024,
        ),
    )(merged, merged, merged, merged, doc_ids.reshape(length, 1), doc_ids.reshape(1, length))
    return (query_out, key_acc.astype(jnp.bfloat16), value_acc.astype(jnp.bfloat16))


def weight_kernel(rows_ref, value_ref, out_ref):
    contract_first = (((0,), (0,)), ((), ()))
    out_ref[...] = lax.dot_general(rows_ref[...], value_ref[...], contract_first,
                                   preferred_element_type=jnp.float32).astype(out_ref.dtype)


def weight_grads(rows, values):
    positions, width = rows.shape
    cols = values.shape[1]
    tile = min(width, 512)
    return pl.pallas_call(
        weight_kernel,
        grid=(width // tile,),
        in_specs=[pl.BlockSpec((positions, tile), lambda i: (0, i)),
                  pl.BlockSpec((positions, cols), lambda i: (0, 0))],
        out_specs=pl.BlockSpec((tile, cols), lambda i: (i, 0)),
        out_shape=jax.ShapeDtypeStruct((width, cols), jnp.bfloat16),
        compiler_params=pltpu.CompilerParams(dimension_semantics=("arbitrary",)),
    )(rows, values)


def local(queries, key_states, section_value_states, out_grad, layer_input, doc_segments):
    section_count = lax.axis_size("section")
    seq_count = lax.axis_size("seq")
    seq_index = lax.axis_index("seq")
    mirror = [(i, section_count - 1 - i) for i in range(section_count)]
    section_index = lax.axis_index("section")
    pair_groups = [
        [s * seq_count + q for q in range(seq_count)]
        + [(section_count - 1 - s) * seq_count + q for q in range(seq_count)]
        for s in range(section_count // 2)
    ]
    pair_rows = lax.all_gather(
        layer_input[0], ("section", "seq"), axis=0, tiled=True, axis_index_groups=pair_groups
    )
    positions = queries.shape[1]
    q_width = queries.shape[2] // seq_count
    k_width = key_states.shape[2] // seq_count
    parts = [
        queries[0].reshape(positions, seq_count, q_width),
        out_grad[0].reshape(positions, seq_count, q_width),
        key_states[0].reshape(positions, seq_count, k_width),
        section_value_states[0].reshape(positions, seq_count, k_width),
    ]
    merged = lax.all_to_all(
        jnp.concatenate(parts, axis=2), "seq", split_axis=1, concat_axis=0, tiled=True
    ).reshape(positions * seq_count, 2 * q_width + 2 * k_width)
    doc_ids = lax.all_to_all(
        jnp.broadcast_to(doc_segments, (seq_count, positions)), "seq",
        split_axis=0, concat_axis=0, tiled=True,
    ).reshape(seq_count * positions)
    query_out, key_out, value_out = attention_grads(merged, doc_ids, q_width, k_width)
    back = lax.all_to_all(
        jnp.concatenate([query_out, key_out], axis=1), "seq", split_axis=0, concat_axis=0,
        tiled=True,
    ).reshape(seq_count, positions, q_width + k_width)
    query_back = jnp.concatenate([back[j, :, :q_width] for j in range(seq_count)], axis=1)
    key_back = jnp.concatenate([back[j, :, q_width:] for j in range(seq_count)], axis=1)
    mirror_value = lax.ppermute(value_out, "section", mirror)
    first_half = section_index < section_count // 2
    pair_values = jnp.where(
        first_half,
        jnp.concatenate([value_out, mirror_value], axis=0),
        jnp.concatenate([mirror_value, value_out], axis=0),
    )
    paired = weight_grads(pair_rows, pair_values)
    return (query_back[None], key_back[None], paired[None])


def solution(mesh):
    in_specs = (
        P("section", "seq", None),
        P("section", "seq", None),
        P("section", "seq", None),
        P("section", "seq", None),
        P("section", "seq", None),
        P("section", "seq"),
    )
    out_specs = (P("section", "seq", None), P("section", "seq", None), P("section", None, "seq"))
    return jax.shard_map(local, mesh=mesh, in_specs=in_specs, out_specs=out_specs, check_vma=False)
```

```python
import math

import jax
import jax.numpy as jnp
from jax import lax
from jax.experimental import pallas as pl
from jax.experimental.pallas import tpu as pltpu
from jax.sharding import PartitionSpec as P

HEAD_WIDTH = 128


def attention_kernel(query_ref, key_ref, value_ref, grad_ref, doc_col_ref, doc_row_ref,
                     query_out_ref, key_out_ref, value_out_ref):
    head, tile = pl.program_id(1), pl.program_id(2)
    rows, length = query_ref.shape[0], key_ref.shape[0]
    scale_factor = 1.0 / math.sqrt(key_ref.shape[1])

    @pl.when((head == 0) & (tile == 0))
    def _():
        key_out_ref[...] = jnp.zeros(key_out_ref.shape, jnp.float32)
        value_out_ref[...] = jnp.zeros(value_out_ref.shape, jnp.float32)

    query_one, grad_one = query_ref[...], grad_ref[...]
    key_col, value_col = key_ref[...], value_ref[...]
    row_pos = tile * rows + lax.broadcasted_iota(jnp.int32, (rows, length), 0)
    col_pos = lax.broadcasted_iota(jnp.int32, (rows, length), 1)
    allowed = (row_pos >= col_pos) & (doc_col_ref[...] == doc_row_ref[...])
    contract_last = (((1,), (1,)), ((), ()))
    contract_first = (((0,), (0,)), ((), ()))
    scores = lax.dot_general(query_one, key_col, contract_last,
                             preferred_element_type=jnp.float32) * scale_factor
    scores = jnp.where(allowed, scores, -jnp.inf)
    row_max = jnp.max(scores, axis=1, keepdims=True)
    weights = jnp.exp(scores - row_max)
    attention = weights / jnp.sum(weights, axis=1, keepdims=True)
    probs_low = attention.astype(jnp.bfloat16)
    attended = jnp.dot(probs_low, value_col, preferred_element_type=jnp.float32).astype(jnp.bfloat16)
    row_delta = jnp.sum(grad_one.astype(jnp.float32) * attended.astype(jnp.float32),
                        axis=1, keepdims=True)
    dprobs = lax.dot_general(grad_one, value_col, contract_last,
                             preferred_element_type=jnp.float32)
    dscores = (attention * (dprobs - row_delta) * scale_factor).astype(jnp.bfloat16)
    query_out_ref[...] = jnp.dot(dscores, key_col,
                                 preferred_element_type=jnp.float32).astype(jnp.bfloat16)
    key_out_ref[...] += lax.dot_general(dscores, query_one, contract_first,
                                        preferred_element_type=jnp.float32)
    value_out_ref[...] += lax.dot_general(probs_low, grad_one, contract_first,
                                          preferred_element_type=jnp.float32)


def attention_grads(merged, doc_ids, q_width, k_width):
    length = merged.shape[0]
    kv_heads = k_width // HEAD_WIDTH
    group_size = q_width // k_width
    rows = min(length, 256)
    tiles = length // rows
    q_blocks, k_blocks = q_width // HEAD_WIDTH, k_width // HEAD_WIDTH

    def head_at(base):
        return pl.BlockSpec((rows, HEAD_WIDTH), lambda g, h, t: (t, base + g * group_size + h))

    def kv_at(base):
        return pl.BlockSpec((length, HEAD_WIDTH), lambda g, h, t: (0, base + g))

    query_out, key_acc, value_acc = pl.pallas_call(
        attention_kernel,
        grid=(kv_heads, group_size, tiles),
        in_specs=[
            head_at(0),
            kv_at(2 * q_blocks),
            kv_at(2 * q_blocks + k_blocks),
            head_at(q_blocks),
            pl.BlockSpec((rows, 1), lambda g, h, t: (t, 0)),
            pl.BlockSpec((1, length), lambda g, h, t: (0, 0)),
        ],
        out_specs=[
            pl.BlockSpec((rows, HEAD_WIDTH), lambda g, h, t: (t, g * group_size + h)),
            kv_at(0),
            kv_at(0),
        ],
        out_shape=[
            jax.ShapeDtypeStruct((length, q_width), jnp.bfloat16),
            jax.ShapeDtypeStruct((length, k_width), jnp.float32),
            jax.ShapeDtypeStruct((length, k_width), jnp.float32),
        ],
        compiler_params=pltpu.CompilerParams(
            dimension_semantics=("arbitrary", "arbitrary", "arbitrary"),
            vmem_limit_bytes=48 * 1024 * 1024,
        ),
    )(merged, merged, merged, merged, doc_ids.reshape(length, 1), doc_ids.reshape(1, length))
    return (query_out, key_acc.astype(jnp.bfloat16), value_acc.astype(jnp.bfloat16))


def weight_kernel(own_ref, mirror_ref, own_value_ref, mirror_value_ref, out_ref):
    contract_first = (((0,), (0,)), ((), ()))
    total = lax.dot_general(own_ref[...], own_value_ref[...], contract_first,
                            preferred_element_type=jnp.float32)
    total = total + lax.dot_general(mirror_ref[...], mirror_value_ref[...], contract_first,
                                    preferred_element_type=jnp.float32)
    out_ref[...] = total.astype(out_ref.dtype)


def weight_grads(own_rows, mirror_rows, own_values, mirror_values):
    positions, width = own_rows.shape
    cols = own_values.shape[1]
    tile = min(width, 512)
    row_spec = pl.BlockSpec((positions, tile), lambda i: (0, i))
    value_spec = pl.BlockSpec((positions, cols), lambda i: (0, 0))
    return pl.pallas_call(
        weight_kernel,
        grid=(width // tile,),
        in_specs=[row_spec, row_spec, value_spec, value_spec],
        out_specs=pl.BlockSpec((tile, cols), lambda i: (i, 0)),
        out_shape=jax.ShapeDtypeStruct((width, cols), jnp.bfloat16),
        compiler_params=pltpu.CompilerParams(dimension_semantics=("arbitrary",)),
    )(own_rows, mirror_rows, own_values, mirror_values)


def local(queries, key_states, section_value_states, out_grad, layer_input, doc_segments):
    section_count = lax.axis_size("section")
    seq_count = lax.axis_size("seq")
    seq_index = lax.axis_index("seq")
    mirror = [(i, section_count - 1 - i) for i in range(section_count)]
    own_rows = layer_input[0]
    own_gathered = lax.all_gather(own_rows, "seq", axis=0, tiled=True)
    mirror_rows = lax.ppermute(own_rows, "section", mirror)
    positions = queries.shape[1]
    q_width = queries.shape[2] // seq_count
    k_width = key_states.shape[2] // seq_count
    parts = [
        queries[0].reshape(positions, seq_count, q_width),
        out_grad[0].reshape(positions, seq_count, q_width),
        key_states[0].reshape(positions, seq_count, k_width),
        section_value_states[0].reshape(positions, seq_count, k_width),
    ]
    merged = lax.all_to_all(
        jnp.concatenate(parts, axis=2), "seq", split_axis=1, concat_axis=0, tiled=True
    ).reshape(positions * seq_count, 2 * q_width + 2 * k_width)
    doc_ids = lax.all_to_all(
        jnp.broadcast_to(doc_segments, (seq_count, positions)), "seq",
        split_axis=0, concat_axis=0, tiled=True,
    ).reshape(seq_count * positions)
    merged, mirror_rows = lax.optimization_barrier((merged, mirror_rows))
    mirror_gathered = lax.all_gather(mirror_rows, "seq", axis=0, tiled=True)
    query_out, key_out, value_out = attention_grads(merged, doc_ids, q_width, k_width)
    back = lax.all_to_all(
        jnp.concatenate([query_out, key_out], axis=1), "seq", split_axis=0, concat_axis=0,
        tiled=True,
    ).reshape(seq_count, positions, q_width + k_width)
    query_back = jnp.concatenate([back[j, :, :q_width] for j in range(seq_count)], axis=1)
    key_back = jnp.concatenate([back[j, :, q_width:] for j in range(seq_count)], axis=1)
    mirror_value = lax.ppermute(value_out, "section", mirror)
    paired = weight_grads(own_gathered, mirror_gathered, value_out, mirror_value)
    return (query_back[None], key_back[None], paired[None])


def solution(mesh):
    in_specs = (
        P("section", "seq", None),
        P("section", "seq", None),
        P("section", "seq", None),
        P("section", "seq", None),
        P("section", "seq", None),
        P("section", "seq"),
    )
    out_specs = (P("section", "seq", None), P("section", "seq", None), P("section", None, "seq"))
    return jax.shard_map(local, mesh=mesh, in_specs=in_specs, out_specs=out_specs, check_vma=False)
```

```python
import math

import jax
import jax.numpy as jnp
from jax import lax
from jax.experimental import pallas as pl
from jax.experimental.pallas import tpu as pltpu
from jax.sharding import PartitionSpec as P

HEAD_WIDTH = 128


def attention_kernel(query_ref, key_ref, value_ref, grad_ref, doc_col_ref, doc_row_ref,
                     query_out_ref, key_out_ref, value_out_ref):
    head, tile = pl.program_id(1), pl.program_id(2)
    rows, length = query_ref.shape[0], key_ref.shape[0]
    scale_factor = 1.0 / math.sqrt(key_ref.shape[1])

    @pl.when((head == 0) & (tile == 0))
    def _():
        key_out_ref[...] = jnp.zeros(key_out_ref.shape, jnp.float32)
        value_out_ref[...] = jnp.zeros(value_out_ref.shape, jnp.float32)

    query_one, grad_one = query_ref[...], grad_ref[...]
    key_col, value_col = key_ref[...], value_ref[...]
    row_pos = tile * rows + lax.broadcasted_iota(jnp.int32, (rows, length), 0)
    col_pos = lax.broadcasted_iota(jnp.int32, (rows, length), 1)
    allowed = (row_pos >= col_pos) & (doc_col_ref[...] == doc_row_ref[...])
    contract_last = (((1,), (1,)), ((), ()))
    contract_first = (((0,), (0,)), ((), ()))
    scores = lax.dot_general(query_one, key_col, contract_last,
                             preferred_element_type=jnp.float32) * scale_factor
    scores = jnp.where(allowed, scores, -jnp.inf)
    row_max = jnp.max(scores, axis=1, keepdims=True)
    weights = jnp.exp(scores - row_max)
    attention = weights / jnp.sum(weights, axis=1, keepdims=True)
    probs_low = attention.astype(jnp.bfloat16)
    attended = jnp.dot(probs_low, value_col, preferred_element_type=jnp.float32).astype(jnp.bfloat16)
    row_delta = jnp.sum(grad_one.astype(jnp.float32) * attended.astype(jnp.float32),
                        axis=1, keepdims=True)
    dprobs = lax.dot_general(grad_one, value_col, contract_last,
                             preferred_element_type=jnp.float32)
    dscores = (attention * (dprobs - row_delta) * scale_factor).astype(jnp.bfloat16)
    query_out_ref[...] = jnp.dot(dscores, key_col,
                                 preferred_element_type=jnp.float32).astype(jnp.bfloat16)
    key_out_ref[...] += lax.dot_general(dscores, query_one, contract_first,
                                        preferred_element_type=jnp.float32)
    value_out_ref[...] += lax.dot_general(probs_low, grad_one, contract_first,
                                          preferred_element_type=jnp.float32)


def attention_grads(merged, doc_ids, q_width, k_width):
    length = merged.shape[0]
    kv_heads = k_width // HEAD_WIDTH
    group_size = q_width // k_width
    rows = min(length, 256)
    tiles = length // rows
    q_blocks, k_blocks = q_width // HEAD_WIDTH, k_width // HEAD_WIDTH

    def head_at(base):
        return pl.BlockSpec((rows, HEAD_WIDTH), lambda g, h, t: (t, base + g * group_size + h))

    def kv_at(base):
        return pl.BlockSpec((length, HEAD_WIDTH), lambda g, h, t: (0, base + g))

    query_out, key_acc, value_acc = pl.pallas_call(
        attention_kernel,
        grid=(kv_heads, group_size, tiles),
        in_specs=[
            head_at(0),
            kv_at(2 * q_blocks),
            kv_at(2 * q_blocks + k_blocks),
            head_at(q_blocks),
            pl.BlockSpec((rows, 1), lambda g, h, t: (t, 0)),
            pl.BlockSpec((1, length), lambda g, h, t: (0, 0)),
        ],
        out_specs=[
            pl.BlockSpec((rows, HEAD_WIDTH), lambda g, h, t: (t, g * group_size + h)),
            kv_at(0),
            kv_at(0),
        ],
        out_shape=[
            jax.ShapeDtypeStruct((length, q_width), jnp.bfloat16),
            jax.ShapeDtypeStruct((length, k_width), jnp.float32),
            jax.ShapeDtypeStruct((length, k_width), jnp.float32),
        ],
        compiler_params=pltpu.CompilerParams(
            dimension_semantics=("arbitrary", "arbitrary", "arbitrary"),
            vmem_limit_bytes=48 * 1024 * 1024,
        ),
    )(merged, merged, merged, merged, doc_ids.reshape(length, 1), doc_ids.reshape(1, length))
    return (query_out, key_acc.astype(jnp.bfloat16), value_acc.astype(jnp.bfloat16))


def weight_kernel(own_ref, mirror_ref, own_value_ref, mirror_value_ref, out_ref):
    contract_first = (((0,), (0,)), ((), ()))
    total = lax.dot_general(own_ref[...], own_value_ref[...], contract_first,
                            preferred_element_type=jnp.float32)
    total = total + lax.dot_general(mirror_ref[...], mirror_value_ref[...], contract_first,
                                    preferred_element_type=jnp.float32)
    out_ref[...] = total.astype(out_ref.dtype)


def weight_grads(own_rows, mirror_rows, own_values, mirror_values):
    positions, width = own_rows.shape
    cols = own_values.shape[1]
    tile = min(width, 512)
    row_spec = pl.BlockSpec((positions, tile), lambda i: (0, i))
    value_spec = pl.BlockSpec((positions, cols), lambda i: (0, 0))
    return pl.pallas_call(
        weight_kernel,
        grid=(width // tile,),
        in_specs=[row_spec, row_spec, value_spec, value_spec],
        out_specs=pl.BlockSpec((tile, cols), lambda i: (i, 0)),
        out_shape=jax.ShapeDtypeStruct((width, cols), jnp.bfloat16),
        compiler_params=pltpu.CompilerParams(dimension_semantics=("arbitrary",)),
    )(own_rows, mirror_rows, own_values, mirror_values)


def local(queries, key_states, section_value_states, out_grad, layer_input, doc_segments):
    section_count = lax.axis_size("section")
    seq_count = lax.axis_size("seq")
    seq_index = lax.axis_index("seq")
    mirror = [(i, section_count - 1 - i) for i in range(section_count)]
    section_index = lax.axis_index("section")
    lower = section_index < section_count // 2
    width = layer_input.shape[2]
    half = width // 2
    own_start = jnp.where(lower, 0, half)
    other_start = jnp.where(lower, half, 0)
    own_half = lax.dynamic_slice_in_dim(layer_input[0], own_start, half, axis=1)
    other_half = lax.dynamic_slice_in_dim(layer_input[0], other_start, half, axis=1)
    own_gathered = lax.all_gather(own_half, "seq", axis=0, tiled=True)
    mirror_rows = lax.ppermute(other_half, "section", mirror)
    positions = queries.shape[1]
    q_width = queries.shape[2] // seq_count
    k_width = key_states.shape[2] // seq_count
    parts = [
        queries[0].reshape(positions, seq_count, q_width),
        out_grad[0].reshape(positions, seq_count, q_width),
        key_states[0].reshape(positions, seq_count, k_width),
        section_value_states[0].reshape(positions, seq_count, k_width),
    ]
    merged = lax.all_to_all(
        jnp.concatenate(parts, axis=2), "seq", split_axis=1, concat_axis=0, tiled=True
    ).reshape(positions * seq_count, 2 * q_width + 2 * k_width)
    doc_ids = lax.all_to_all(
        jnp.broadcast_to(doc_segments, (seq_count, positions)), "seq",
        split_axis=0, concat_axis=0, tiled=True,
    ).reshape(seq_count * positions)
    merged, mirror_rows = lax.optimization_barrier((merged, mirror_rows))
    mirror_gathered = lax.all_gather(mirror_rows, "seq", axis=0, tiled=True)
    query_out, key_out, value_out = attention_grads(merged, doc_ids, q_width, k_width)
    back = lax.all_to_all(
        jnp.concatenate([query_out, key_out], axis=1), "seq", split_axis=0, concat_axis=0,
        tiled=True,
    ).reshape(seq_count, positions, q_width + k_width)
    query_back = jnp.concatenate([back[j, :, :q_width] for j in range(seq_count)], axis=1)
    key_back = jnp.concatenate([back[j, :, q_width:] for j in range(seq_count)], axis=1)
    mirror_value = lax.ppermute(value_out, "section", mirror)
    mine = weight_grads(own_gathered, mirror_gathered, value_out, mirror_value)
    theirs = lax.ppermute(mine, "section", mirror)
    paired = jnp.concatenate(
        [jnp.where(lower, mine, theirs), jnp.where(lower, theirs, mine)], axis=0
    )
    return (query_back[None], key_back[None], paired[None])


def solution(mesh):
    in_specs = (
        P("section", "seq", None),
        P("section", "seq", None),
        P("section", "seq", None),
        P("section", "seq", None),
        P("section", "seq", None),
        P("section", "seq"),
    )
    out_specs = (P("section", "seq", None), P("section", "seq", None), P("section", None, "seq"))
    return jax.shard_map(local, mesh=mesh, in_specs=in_specs, out_specs=out_specs, check_vma=False)
```

```python
import math

import jax
import jax.numpy as jnp
from jax import lax
from jax.experimental import pallas as pl
from jax.experimental.pallas import tpu as pltpu
from jax.sharding import PartitionSpec as P

HEAD_WIDTH = 128


def attention_kernel(query_ref, key_ref, value_ref, grad_ref, doc_col_ref, doc_row_ref,
                     query_out_ref, key_out_ref, value_out_ref):
    head, tile = pl.program_id(1), pl.program_id(2)
    rows, length = query_ref.shape[0], key_ref.shape[0]
    scale_factor = 1.0 / math.sqrt(key_ref.shape[1])

    @pl.when((head == 0) & (tile == 0))
    def _():
        key_out_ref[...] = jnp.zeros(key_out_ref.shape, jnp.float32)
        value_out_ref[...] = jnp.zeros(value_out_ref.shape, jnp.float32)

    query_one, grad_one = query_ref[...], grad_ref[...]
    key_col, value_col = key_ref[...], value_ref[...]
    row_pos = tile * rows + lax.broadcasted_iota(jnp.int32, (rows, length), 0)
    col_pos = lax.broadcasted_iota(jnp.int32, (rows, length), 1)
    allowed = (row_pos >= col_pos) & (doc_col_ref[...] == doc_row_ref[...])
    contract_last = (((1,), (1,)), ((), ()))
    contract_first = (((0,), (0,)), ((), ()))
    scores = lax.dot_general(query_one, key_col, contract_last,
                             preferred_element_type=jnp.float32) * scale_factor
    scores = jnp.where(allowed, scores, -jnp.inf)
    row_max = jnp.max(scores, axis=1, keepdims=True)
    weights = jnp.exp(scores - row_max)
    attention = weights / jnp.sum(weights, axis=1, keepdims=True)
    probs_low = attention.astype(jnp.bfloat16)
    attended = jnp.dot(probs_low, value_col, preferred_element_type=jnp.float32).astype(jnp.bfloat16)
    row_delta = jnp.sum(grad_one.astype(jnp.float32) * attended.astype(jnp.float32),
                        axis=1, keepdims=True)
    dprobs = lax.dot_general(grad_one, value_col, contract_last,
                             preferred_element_type=jnp.float32)
    dscores = (attention * (dprobs - row_delta) * scale_factor).astype(jnp.bfloat16)
    query_out_ref[...] = jnp.dot(dscores, key_col,
                                 preferred_element_type=jnp.float32).astype(jnp.bfloat16)
    key_out_ref[...] += lax.dot_general(dscores, query_one, contract_first,
                                        preferred_element_type=jnp.float32)
    value_out_ref[...] += lax.dot_general(probs_low, grad_one, contract_first,
                                          preferred_element_type=jnp.float32)


def attention_grads(merged, doc_ids, q_width, k_width):
    length = merged.shape[0]
    kv_heads = k_width // HEAD_WIDTH
    group_size = q_width // k_width
    rows = min(length, 256)
    tiles = length // rows
    q_blocks, k_blocks = q_width // HEAD_WIDTH, k_width // HEAD_WIDTH

    def head_at(base):
        return pl.BlockSpec((rows, HEAD_WIDTH), lambda g, h, t: (t, base + g * group_size + h))

    def kv_at(base):
        return pl.BlockSpec((length, HEAD_WIDTH), lambda g, h, t: (0, base + g))

    query_out, key_acc, value_acc = pl.pallas_call(
        attention_kernel,
        grid=(kv_heads, group_size, tiles),
        in_specs=[
            head_at(0),
            kv_at(2 * q_blocks),
            kv_at(2 * q_blocks + k_blocks),
            head_at(q_blocks),
            pl.BlockSpec((rows, 1), lambda g, h, t: (t, 0)),
            pl.BlockSpec((1, length), lambda g, h, t: (0, 0)),
        ],
        out_specs=[
            pl.BlockSpec((rows, HEAD_WIDTH), lambda g, h, t: (t, g * group_size + h)),
            kv_at(0),
            kv_at(0),
        ],
        out_shape=[
            jax.ShapeDtypeStruct((length, q_width), jnp.bfloat16),
            jax.ShapeDtypeStruct((length, k_width), jnp.float32),
            jax.ShapeDtypeStruct((length, k_width), jnp.float32),
        ],
        compiler_params=pltpu.CompilerParams(
            dimension_semantics=("arbitrary", "arbitrary", "arbitrary"),
            vmem_limit_bytes=48 * 1024 * 1024,
        ),
    )(merged, merged, merged, merged, doc_ids.reshape(length, 1), doc_ids.reshape(1, length))
    return (query_out, key_acc.astype(jnp.bfloat16), value_acc.astype(jnp.bfloat16))


def weight_kernel(own_ref, mirror_ref, own_value_ref, mirror_value_ref, out_ref):
    contract_first = (((0,), (0,)), ((), ()))
    total = lax.dot_general(own_ref[...], own_value_ref[...], contract_first,
                            preferred_element_type=jnp.float32)
    total = total + lax.dot_general(mirror_ref[...], mirror_value_ref[...], contract_first,
                                    preferred_element_type=jnp.float32)
    out_ref[...] = total.astype(out_ref.dtype)


def weight_grads(own_rows, mirror_rows, own_values, mirror_values):
    positions, width = own_rows.shape
    cols = own_values.shape[1]
    tile = min(width, 512)
    row_spec = pl.BlockSpec((positions, tile), lambda i: (0, i))
    value_spec = pl.BlockSpec((positions, cols), lambda i: (0, 0))
    return pl.pallas_call(
        weight_kernel,
        grid=(width // tile,),
        in_specs=[row_spec, row_spec, value_spec, value_spec],
        out_specs=pl.BlockSpec((tile, cols), lambda i: (i, 0)),
        out_shape=jax.ShapeDtypeStruct((width, cols), jnp.bfloat16),
        compiler_params=pltpu.CompilerParams(dimension_semantics=("arbitrary",)),
    )(own_rows, mirror_rows, own_values, mirror_values)


def local(queries, key_states, section_value_states, out_grad, layer_input, doc_segments):
    section_count = lax.axis_size("section")
    seq_count = lax.axis_size("seq")
    seq_index = lax.axis_index("seq")
    mirror = [(i, section_count - 1 - i) for i in range(section_count)]
    own_rows = layer_input[0]
    own_gathered = lax.all_gather(own_rows, "seq", axis=0, tiled=True)
    mirror_rows = lax.ppermute(own_rows, "section", mirror)
    positions = queries.shape[1]
    q_width = queries.shape[2] // seq_count
    k_width = key_states.shape[2] // seq_count
    parts = [
        queries[0].reshape(positions, seq_count, q_width),
        out_grad[0].reshape(positions, seq_count, q_width),
        key_states[0].reshape(positions, seq_count, k_width),
        section_value_states[0].reshape(positions, seq_count, k_width),
    ]
    merged = lax.all_to_all(
        jnp.concatenate(parts, axis=2), "seq", split_axis=1, concat_axis=0, tiled=True
    ).reshape(positions * seq_count, 2 * q_width + 2 * k_width)
    doc_ids = lax.all_to_all(
        jnp.broadcast_to(doc_segments, (seq_count, positions)), "seq",
        split_axis=0, concat_axis=0, tiled=True,
    ).reshape(seq_count * positions)
    merged, mirror_rows = lax.optimization_barrier((merged, mirror_rows))
    mirror_gathered = lax.all_to_all(
        jnp.broadcast_to(mirror_rows, (seq_count,) + mirror_rows.shape), "seq",
        split_axis=0, concat_axis=0, tiled=True,
    ).reshape(seq_count * mirror_rows.shape[0], mirror_rows.shape[1])
    query_out, key_out, value_out = attention_grads(merged, doc_ids, q_width, k_width)
    back = lax.all_to_all(
        jnp.concatenate([query_out, key_out], axis=1), "seq", split_axis=0, concat_axis=0,
        tiled=True,
    ).reshape(seq_count, positions, q_width + k_width)
    query_back = jnp.concatenate([back[j, :, :q_width] for j in range(seq_count)], axis=1)
    key_back = jnp.concatenate([back[j, :, q_width:] for j in range(seq_count)], axis=1)
    mirror_value = lax.ppermute(value_out, "section", mirror)
    paired = weight_grads(own_gathered, mirror_gathered, value_out, mirror_value)
    return (query_back[None], key_back[None], paired[None])


def solution(mesh):
    in_specs = (
        P("section", "seq", None),
        P("section", "seq", None),
        P("section", "seq", None),
        P("section", "seq", None),
        P("section", "seq", None),
        P("section", "seq"),
    )
    out_specs = (P("section", "seq", None), P("section", "seq", None), P("section", None, "seq"))
    return jax.shard_map(local, mesh=mesh, in_specs=in_specs, out_specs=out_specs, check_vma=False)
```

```python
import math

import jax
import jax.numpy as jnp
from jax import lax
from jax.experimental import pallas as pl
from jax.experimental.pallas import tpu as pltpu
from jax.sharding import PartitionSpec as P

HEAD_WIDTH = 128


def attention_kernel(query_ref, key_ref, value_ref, grad_ref, doc_col_ref, doc_row_ref,
                     query_out_ref, key_out_ref, value_out_ref):
    head, tile = pl.program_id(1), pl.program_id(2)
    rows, length = query_ref.shape[0], key_ref.shape[0]
    scale_factor = 1.0 / math.sqrt(key_ref.shape[1])

    @pl.when((head == 0) & (tile == 0))
    def _():
        key_out_ref[...] = jnp.zeros(key_out_ref.shape, jnp.float32)
        value_out_ref[...] = jnp.zeros(value_out_ref.shape, jnp.float32)

    query_one, grad_one = query_ref[...], grad_ref[...]
    key_col, value_col = key_ref[...], value_ref[...]
    row_pos = tile * rows + lax.broadcasted_iota(jnp.int32, (rows, length), 0)
    col_pos = lax.broadcasted_iota(jnp.int32, (rows, length), 1)
    allowed = (row_pos >= col_pos) & (doc_col_ref[...] == doc_row_ref[...])
    contract_last = (((1,), (1,)), ((), ()))
    contract_first = (((0,), (0,)), ((), ()))
    scores = lax.dot_general(query_one, key_col, contract_last,
                             preferred_element_type=jnp.float32) * scale_factor
    scores = jnp.where(allowed, scores, -jnp.inf)
    row_max = jnp.max(scores, axis=1, keepdims=True)
    weights = jnp.exp(scores - row_max)
    attention = weights / jnp.sum(weights, axis=1, keepdims=True)
    probs_low = attention.astype(jnp.bfloat16)
    attended = jnp.dot(probs_low, value_col, preferred_element_type=jnp.float32).astype(jnp.bfloat16)
    row_delta = jnp.sum(grad_one.astype(jnp.float32) * attended.astype(jnp.float32),
                        axis=1, keepdims=True)
    dprobs = lax.dot_general(grad_one, value_col, contract_last,
                             preferred_element_type=jnp.float32)
    dscores = (attention * (dprobs - row_delta) * scale_factor).astype(jnp.bfloat16)
    query_out_ref[...] = jnp.dot(dscores, key_col,
                                 preferred_element_type=jnp.float32).astype(jnp.bfloat16)
    key_out_ref[...] += lax.dot_general(dscores, query_one, contract_first,
                                        preferred_element_type=jnp.float32)
    value_out_ref[...] += lax.dot_general(probs_low, grad_one, contract_first,
                                          preferred_element_type=jnp.float32)


def attention_grads(merged, doc_ids, q_width, k_width):
    length = merged.shape[0]
    kv_heads = k_width // HEAD_WIDTH
    group_size = q_width // k_width
    rows = min(length, 256)
    tiles = length // rows
    q_blocks, k_blocks = q_width // HEAD_WIDTH, k_width // HEAD_WIDTH

    def head_at(base):
        return pl.BlockSpec((rows, HEAD_WIDTH), lambda g, h, t: (t, base + g * group_size + h))

    def kv_at(base):
        return pl.BlockSpec((length, HEAD_WIDTH), lambda g, h, t: (0, base + g))

    query_out, key_acc, value_acc = pl.pallas_call(
        attention_kernel,
        grid=(kv_heads, group_size, tiles),
        in_specs=[
            head_at(0),
            kv_at(2 * q_blocks),
            kv_at(2 * q_blocks + k_blocks),
            head_at(q_blocks),
            pl.BlockSpec((rows, 1), lambda g, h, t: (t, 0)),
            pl.BlockSpec((1, length), lambda g, h, t: (0, 0)),
        ],
        out_specs=[
            pl.BlockSpec((rows, HEAD_WIDTH), lambda g, h, t: (t, g * group_size + h)),
            kv_at(0),
            kv_at(0),
        ],
        out_shape=[
            jax.ShapeDtypeStruct((length, q_width), jnp.bfloat16),
            jax.ShapeDtypeStruct((length, k_width), jnp.float32),
            jax.ShapeDtypeStruct((length, k_width), jnp.float32),
        ],
        compiler_params=pltpu.CompilerParams(
            dimension_semantics=("arbitrary", "arbitrary", "arbitrary"),
            vmem_limit_bytes=48 * 1024 * 1024,
        ),
    )(merged, merged, merged, merged, doc_ids.reshape(length, 1), doc_ids.reshape(1, length))
    return (query_out, key_acc.astype(jnp.bfloat16), value_acc.astype(jnp.bfloat16))


def weight_kernel(own_ref, mirror_ref, own_value_ref, mirror_value_ref, out_ref):
    contract_first = (((0,), (0,)), ((), ()))
    total = lax.dot_general(own_ref[...], own_value_ref[...], contract_first,
                            preferred_element_type=jnp.float32)
    total = total + lax.dot_general(mirror_ref[...], mirror_value_ref[...], contract_first,
                                    preferred_element_type=jnp.float32)
    out_ref[...] = total.astype(out_ref.dtype)


def weight_grads(own_rows, mirror_rows, own_values, mirror_values):
    positions, width = own_rows.shape
    cols = own_values.shape[1]
    tile = min(width, 512)
    row_spec = pl.BlockSpec((positions, tile), lambda i: (0, i))
    value_spec = pl.BlockSpec((positions, cols), lambda i: (0, 0))
    return pl.pallas_call(
        weight_kernel,
        grid=(width // tile,),
        in_specs=[row_spec, row_spec, value_spec, value_spec],
        out_specs=pl.BlockSpec((tile, cols), lambda i: (i, 0)),
        out_shape=jax.ShapeDtypeStruct((width, cols), jnp.bfloat16),
        compiler_params=pltpu.CompilerParams(dimension_semantics=("arbitrary",)),
    )(own_rows, mirror_rows, own_values, mirror_values)


def local(queries, key_states, section_value_states, out_grad, layer_input, doc_segments):
    section_count = lax.axis_size("section")
    seq_count = lax.axis_size("seq")
    seq_index = lax.axis_index("seq")
    mirror = [(i, section_count - 1 - i) for i in range(section_count)]
    section_index = lax.axis_index("section")
    lower = section_index < section_count // 2
    width = layer_input.shape[2]
    span = width - width // 4
    rest = width - span
    own_start = jnp.where(lower, 0, rest)
    other_start = jnp.where(lower, rest, 0)
    own_half = lax.dynamic_slice_in_dim(layer_input[0], own_start, span, axis=1)
    other_half = lax.dynamic_slice_in_dim(layer_input[0], other_start, span, axis=1)
    own_gathered = lax.all_gather(own_half, "seq", axis=0, tiled=True)
    mirror_rows = lax.ppermute(other_half, "section", mirror)
    positions = queries.shape[1]
    q_width = queries.shape[2] // seq_count
    k_width = key_states.shape[2] // seq_count
    parts = [
        queries[0].reshape(positions, seq_count, q_width),
        out_grad[0].reshape(positions, seq_count, q_width),
        key_states[0].reshape(positions, seq_count, k_width),
        section_value_states[0].reshape(positions, seq_count, k_width),
    ]
    merged = lax.all_to_all(
        jnp.concatenate(parts, axis=2), "seq", split_axis=1, concat_axis=0, tiled=True
    ).reshape(positions * seq_count, 2 * q_width + 2 * k_width)
    doc_ids = lax.all_to_all(
        jnp.broadcast_to(doc_segments, (seq_count, positions)), "seq",
        split_axis=0, concat_axis=0, tiled=True,
    ).reshape(seq_count * positions)
    merged, mirror_rows = lax.optimization_barrier((merged, mirror_rows))
    mirror_gathered = lax.all_gather(mirror_rows, "seq", axis=0, tiled=True)
    query_out, key_out, value_out = attention_grads(merged, doc_ids, q_width, k_width)
    back = lax.all_to_all(
        jnp.concatenate([query_out, key_out], axis=1), "seq", split_axis=0, concat_axis=0,
        tiled=True,
    ).reshape(seq_count, positions, q_width + k_width)
    query_back = jnp.concatenate([back[j, :, :q_width] for j in range(seq_count)], axis=1)
    key_back = jnp.concatenate([back[j, :, q_width:] for j in range(seq_count)], axis=1)
    mirror_value = lax.ppermute(value_out, "section", mirror)
    mine = weight_grads(own_gathered, mirror_gathered, value_out, mirror_value)
    shared = lax.dynamic_slice_in_dim(mine, jnp.where(lower, 0, span - rest), rest, axis=0)
    theirs = lax.ppermute(shared, "section", mirror)
    paired = jnp.where(
        lower,
        jnp.concatenate([mine, theirs], axis=0),
        jnp.concatenate([theirs, mine], axis=0),
    )
    return (query_back[None], key_back[None], paired[None])


def solution(mesh):
    in_specs = (
        P("section", "seq", None),
        P("section", "seq", None),
        P("section", "seq", None),
        P("section", "seq", None),
        P("section", "seq", None),
        P("section", "seq"),
    )
    out_specs = (P("section", "seq", None), P("section", "seq", None), P("section", None, "seq"))
    return jax.shard_map(local, mesh=mesh, in_specs=in_specs, out_specs=out_specs, check_vma=False)
```

```python
import math

import jax
import jax.numpy as jnp
from jax import lax
from jax.experimental import pallas as pl
from jax.experimental.pallas import tpu as pltpu
from jax.sharding import PartitionSpec as P

HEAD_WIDTH = 128


def attention_kernel(query_ref, key_ref, value_ref, grad_ref, doc_col_ref, doc_row_ref,
                     query_out_ref, key_out_ref, value_out_ref):
    head, tile = pl.program_id(1), pl.program_id(2)
    rows, length = query_ref.shape[0], key_ref.shape[0]
    scale_factor = 1.0 / math.sqrt(key_ref.shape[1])

    @pl.when((head == 0) & (tile == 0))
    def _():
        key_out_ref[...] = jnp.zeros(key_out_ref.shape, jnp.float32)
        value_out_ref[...] = jnp.zeros(value_out_ref.shape, jnp.float32)

    query_one, grad_one = query_ref[...], grad_ref[...]
    key_col, value_col = key_ref[...], value_ref[...]
    row_pos = tile * rows + lax.broadcasted_iota(jnp.int32, (rows, length), 0)
    col_pos = lax.broadcasted_iota(jnp.int32, (rows, length), 1)
    allowed = (row_pos >= col_pos) & (doc_col_ref[...] == doc_row_ref[...])
    contract_last = (((1,), (1,)), ((), ()))
    contract_first = (((0,), (0,)), ((), ()))
    scores = lax.dot_general(query_one, key_col, contract_last,
                             preferred_element_type=jnp.float32) * scale_factor
    scores = jnp.where(allowed, scores, -jnp.inf)
    row_max = jnp.max(scores, axis=1, keepdims=True)
    weights = jnp.exp(scores - row_max)
    attention = weights / jnp.sum(weights, axis=1, keepdims=True)
    probs_low = attention.astype(jnp.bfloat16)
    attended = jnp.dot(probs_low, value_col, preferred_element_type=jnp.float32).astype(jnp.bfloat16)
    row_delta = jnp.sum(grad_one.astype(jnp.float32) * attended.astype(jnp.float32),
                        axis=1, keepdims=True)
    dprobs = lax.dot_general(grad_one, value_col, contract_last,
                             preferred_element_type=jnp.float32)
    dscores = (attention * (dprobs - row_delta) * scale_factor).astype(jnp.bfloat16)
    query_out_ref[...] = jnp.dot(dscores, key_col,
                                 preferred_element_type=jnp.float32).astype(jnp.bfloat16)
    key_out_ref[...] += lax.dot_general(dscores, query_one, contract_first,
                                        preferred_element_type=jnp.float32)
    value_out_ref[...] += lax.dot_general(probs_low, grad_one, contract_first,
                                          preferred_element_type=jnp.float32)


def attention_grads(merged, doc_ids, q_width, k_width):
    length = merged.shape[0]
    kv_heads = k_width // HEAD_WIDTH
    group_size = q_width // k_width
    rows = min(length, 256)
    tiles = length // rows
    q_blocks, k_blocks = q_width // HEAD_WIDTH, k_width // HEAD_WIDTH

    def head_at(base):
        return pl.BlockSpec((rows, HEAD_WIDTH), lambda g, h, t: (t, base + g * group_size + h))

    def kv_at(base):
        return pl.BlockSpec((length, HEAD_WIDTH), lambda g, h, t: (0, base + g))

    query_out, key_acc, value_acc = pl.pallas_call(
        attention_kernel,
        grid=(kv_heads, group_size, tiles),
        in_specs=[
            head_at(0),
            kv_at(2 * q_blocks),
            kv_at(2 * q_blocks + k_blocks),
            head_at(q_blocks),
            pl.BlockSpec((rows, 1), lambda g, h, t: (t, 0)),
            pl.BlockSpec((1, length), lambda g, h, t: (0, 0)),
        ],
        out_specs=[
            pl.BlockSpec((rows, HEAD_WIDTH), lambda g, h, t: (t, g * group_size + h)),
            kv_at(0),
            kv_at(0),
        ],
        out_shape=[
            jax.ShapeDtypeStruct((length, q_width), jnp.bfloat16),
            jax.ShapeDtypeStruct((length, k_width), jnp.float32),
            jax.ShapeDtypeStruct((length, k_width), jnp.float32),
        ],
        compiler_params=pltpu.CompilerParams(
            dimension_semantics=("arbitrary", "arbitrary", "arbitrary"),
            vmem_limit_bytes=48 * 1024 * 1024,
        ),
    )(merged, merged, merged, merged, doc_ids.reshape(length, 1), doc_ids.reshape(1, length))
    return (query_out, key_acc.astype(jnp.bfloat16), value_acc.astype(jnp.bfloat16))


def partial_kernel(rows_ref, value_ref, out_ref):
    contract_first = (((0,), (0,)), ((), ()))
    out_ref[...] = lax.dot_general(rows_ref[...], value_ref[...], contract_first,
                                   preferred_element_type=jnp.float32)


def weight_kernel(rows_ref, value_ref, partial_ref, out_ref):
    contract_first = (((0,), (0,)), ((), ()))
    total = partial_ref[...] + lax.dot_general(rows_ref[...], value_ref[...], contract_first,
                                               preferred_element_type=jnp.float32)
    out_ref[...] = total.astype(out_ref.dtype)


def weight_grads(own_rows, mirror_rows, own_values, mirror_values):
    positions, width = own_rows.shape
    cols = own_values.shape[1]
    tile = min(width, 512)
    row_spec = pl.BlockSpec((positions, tile), lambda i: (0, i))
    value_spec = pl.BlockSpec((positions, cols), lambda i: (0, 0))
    out_spec = pl.BlockSpec((tile, cols), lambda i: (i, 0))
    params = pltpu.CompilerParams(dimension_semantics=("arbitrary",))
    partial = pl.pallas_call(
        partial_kernel,
        grid=(width // tile,),
        in_specs=[row_spec, value_spec],
        out_specs=out_spec,
        out_shape=jax.ShapeDtypeStruct((width, cols), jnp.float32),
        compiler_params=params,
    )(own_rows, own_values)
    return pl.pallas_call(
        weight_kernel,
        grid=(width // tile,),
        in_specs=[row_spec, value_spec, out_spec],
        out_specs=out_spec,
        out_shape=jax.ShapeDtypeStruct((width, cols), jnp.bfloat16),
        compiler_params=params,
    )(mirror_rows, mirror_values, partial)


def local(queries, key_states, section_value_states, out_grad, layer_input, doc_segments):
    section_count = lax.axis_size("section")
    seq_count = lax.axis_size("seq")
    seq_index = lax.axis_index("seq")
    mirror = [(i, section_count - 1 - i) for i in range(section_count)]
    own_rows = layer_input[0]
    own_gathered = lax.all_gather(own_rows, "seq", axis=0, tiled=True)
    mirror_rows = lax.ppermute(own_rows, "section", mirror)
    positions = queries.shape[1]
    q_width = queries.shape[2] // seq_count
    k_width = key_states.shape[2] // seq_count
    parts = [
        queries[0].reshape(positions, seq_count, q_width),
        out_grad[0].reshape(positions, seq_count, q_width),
        key_states[0].reshape(positions, seq_count, k_width),
        section_value_states[0].reshape(positions, seq_count, k_width),
    ]
    merged = lax.all_to_all(
        jnp.concatenate(parts, axis=2), "seq", split_axis=1, concat_axis=0, tiled=True
    ).reshape(positions * seq_count, 2 * q_width + 2 * k_width)
    doc_ids = lax.all_to_all(
        jnp.broadcast_to(doc_segments, (seq_count, positions)), "seq",
        split_axis=0, concat_axis=0, tiled=True,
    ).reshape(seq_count * positions)
    merged, mirror_rows = lax.optimization_barrier((merged, mirror_rows))
    mirror_gathered = lax.all_gather(mirror_rows, "seq", axis=0, tiled=True)
    query_out, key_out, value_out = attention_grads(merged, doc_ids, q_width, k_width)
    back = lax.all_to_all(
        jnp.concatenate([query_out, key_out], axis=1), "seq", split_axis=0, concat_axis=0,
        tiled=True,
    ).reshape(seq_count, positions, q_width + k_width)
    query_back = jnp.concatenate([back[j, :, :q_width] for j in range(seq_count)], axis=1)
    key_back = jnp.concatenate([back[j, :, q_width:] for j in range(seq_count)], axis=1)
    mirror_value = lax.ppermute(value_out, "section", mirror)
    paired = weight_grads(own_gathered, mirror_gathered, value_out, mirror_value)
    return (query_back[None], key_back[None], paired[None])


def solution(mesh):
    in_specs = (
        P("section", "seq", None),
        P("section", "seq", None),
        P("section", "seq", None),
        P("section", "seq", None),
        P("section", "seq", None),
        P("section", "seq"),
    )
    out_specs = (P("section", "seq", None), P("section", "seq", None), P("section", None, "seq"))
    return jax.shard_map(local, mesh=mesh, in_specs=in_specs, out_specs=out_specs, check_vma=False)
```

```python
import math

import jax
import jax.numpy as jnp
from jax import lax
from jax.experimental import pallas as pl
from jax.experimental.pallas import tpu as pltpu
from jax.sharding import PartitionSpec as P

HEAD_WIDTH = 128


def attention_kernel(query_ref, key_ref, value_ref, grad_ref, doc_col_ref, doc_row_ref,
                     query_out_ref, key_out_ref, value_out_ref):
    head, tile = pl.program_id(1), pl.program_id(2)
    rows, length = query_ref.shape[0], key_ref.shape[0]
    scale_factor = 1.0 / math.sqrt(key_ref.shape[1])

    @pl.when((head == 0) & (tile == 0))
    def _():
        key_out_ref[...] = jnp.zeros(key_out_ref.shape, jnp.float32)
        value_out_ref[...] = jnp.zeros(value_out_ref.shape, jnp.float32)

    query_one, grad_one = query_ref[...], grad_ref[...]
    key_col, value_col = key_ref[...], value_ref[...]
    row_pos = tile * rows + lax.broadcasted_iota(jnp.int32, (rows, length), 0)
    col_pos = lax.broadcasted_iota(jnp.int32, (rows, length), 1)
    allowed = (row_pos >= col_pos) & (doc_col_ref[...] == doc_row_ref[...])
    contract_last = (((1,), (1,)), ((), ()))
    contract_first = (((0,), (0,)), ((), ()))
    scores = lax.dot_general(query_one, key_col, contract_last,
                             preferred_element_type=jnp.float32) * scale_factor
    scores = jnp.where(allowed, scores, -jnp.inf)
    row_max = jnp.max(scores, axis=1, keepdims=True)
    weights = jnp.exp(scores - row_max)
    attention = weights / jnp.sum(weights, axis=1, keepdims=True)
    probs_low = attention.astype(jnp.bfloat16)
    attended = jnp.dot(probs_low, value_col, preferred_element_type=jnp.float32).astype(jnp.bfloat16)
    row_delta = jnp.sum(grad_one.astype(jnp.float32) * attended.astype(jnp.float32),
                        axis=1, keepdims=True)
    dprobs = lax.dot_general(grad_one, value_col, contract_last,
                             preferred_element_type=jnp.float32)
    dscores = (attention * (dprobs - row_delta) * scale_factor).astype(jnp.bfloat16)
    query_out_ref[...] = jnp.dot(dscores, key_col,
                                 preferred_element_type=jnp.float32).astype(jnp.bfloat16)
    key_out_ref[...] += lax.dot_general(dscores, query_one, contract_first,
                                        preferred_element_type=jnp.float32)
    value_out_ref[...] += lax.dot_general(probs_low, grad_one, contract_first,
                                          preferred_element_type=jnp.float32)


def attention_grads(merged, doc_ids, q_width, k_width):
    length = merged.shape[0]
    kv_heads = k_width // HEAD_WIDTH
    group_size = q_width // k_width
    rows = min(length, 256)
    tiles = length // rows
    q_blocks, k_blocks = q_width // HEAD_WIDTH, k_width // HEAD_WIDTH

    def head_at(base):
        return pl.BlockSpec((rows, HEAD_WIDTH), lambda g, h, t: (t, base + g * group_size + h))

    def kv_at(base):
        return pl.BlockSpec((length, HEAD_WIDTH), lambda g, h, t: (0, base + g))

    query_out, key_acc, value_acc = pl.pallas_call(
        attention_kernel,
        grid=(kv_heads, group_size, tiles),
        in_specs=[
            head_at(0),
            kv_at(2 * q_blocks),
            kv_at(2 * q_blocks + k_blocks),
            head_at(q_blocks),
            pl.BlockSpec((rows, 1), lambda g, h, t: (t, 0)),
            pl.BlockSpec((1, length), lambda g, h, t: (0, 0)),
        ],
        out_specs=[
            pl.BlockSpec((rows, HEAD_WIDTH), lambda g, h, t: (t, g * group_size + h)),
            kv_at(0),
            kv_at(0),
        ],
        out_shape=[
            jax.ShapeDtypeStruct((length, q_width), jnp.bfloat16),
            jax.ShapeDtypeStruct((length, k_width), jnp.float32),
            jax.ShapeDtypeStruct((length, k_width), jnp.float32),
        ],
        compiler_params=pltpu.CompilerParams(
            dimension_semantics=("arbitrary", "arbitrary", "arbitrary"),
            vmem_limit_bytes=48 * 1024 * 1024,
        ),
    )(merged, merged, merged, merged, doc_ids.reshape(length, 1), doc_ids.reshape(1, length))
    return (query_out, key_acc.astype(jnp.bfloat16), value_acc.astype(jnp.bfloat16))


def weight_kernel(own_a, own_b, mirror_a, mirror_b, own_value_ref, mirror_value_ref, out_ref):
    contract_first = (((0,), (0,)), ((), ()))
    for slot, (own_ref, mirror_ref) in enumerate(((own_a, mirror_a), (own_b, mirror_b))):
        total = lax.dot_general(own_ref[...], own_value_ref[...], contract_first,
                                preferred_element_type=jnp.float32)
        total = total + lax.dot_general(mirror_ref[...], mirror_value_ref[...], contract_first,
                                        preferred_element_type=jnp.float32)
        out_ref[slot] = total.astype(out_ref.dtype)


def weight_grads(own_parts, mirror_parts, own_values, mirror_values):
    positions, width = own_parts[0].shape
    cols = own_values.shape[1]
    tile = min(width, 512)
    row_spec = pl.BlockSpec((positions, tile), lambda i: (0, i))
    value_spec = pl.BlockSpec((positions, cols), lambda i: (0, 0))
    out = pl.pallas_call(
        weight_kernel,
        grid=(width // tile,),
        in_specs=[row_spec] * 4 + [value_spec, value_spec],
        out_specs=pl.BlockSpec((2, tile, cols), lambda i: (0, i, 0)),
        out_shape=jax.ShapeDtypeStruct((2, width, cols), jnp.bfloat16),
        compiler_params=pltpu.CompilerParams(dimension_semantics=("arbitrary",)),
    )(*own_parts, *mirror_parts, own_values, mirror_values)
    return out.reshape(2 * width, cols)


def column_halves(rows):
    half = rows.shape[1] // 2
    return [rows[:, :half], rows[:, half:]]


def local(queries, key_states, section_value_states, out_grad, layer_input, doc_segments):
    section_count = lax.axis_size("section")
    seq_count = lax.axis_size("seq")
    seq_index = lax.axis_index("seq")
    mirror = [(i, section_count - 1 - i) for i in range(section_count)]
    own_rows = layer_input[0]
    own_gathered = [
        lax.all_gather(part, "seq", axis=0, tiled=True) for part in column_halves(own_rows)
    ]
    mirror_rows = lax.ppermute(own_rows, "section", mirror)
    positions = queries.shape[1]
    q_width = queries.shape[2] // seq_count
    k_width = key_states.shape[2] // seq_count
    parts = [
        queries[0].reshape(positions, seq_count, q_width),
        out_grad[0].reshape(positions, seq_count, q_width),
        key_states[0].reshape(positions, seq_count, k_width),
        section_value_states[0].reshape(positions, seq_count, k_width),
    ]
    merged = lax.all_to_all(
        jnp.concatenate(parts, axis=2), "seq", split_axis=1, concat_axis=0, tiled=True
    ).reshape(positions * seq_count, 2 * q_width + 2 * k_width)
    doc_ids = lax.all_to_all(
        jnp.broadcast_to(doc_segments, (seq_count, positions)), "seq",
        split_axis=0, concat_axis=0, tiled=True,
    ).reshape(seq_count * positions)
    merged, mirror_rows = lax.optimization_barrier((merged, mirror_rows))
    mirror_gathered = [
        lax.all_gather(part, "seq", axis=0, tiled=True) for part in column_halves(mirror_rows)
    ]
    query_out, key_out, value_out = attention_grads(merged, doc_ids, q_width, k_width)
    back = lax.all_to_all(
        jnp.concatenate([query_out, key_out], axis=1), "seq", split_axis=0, concat_axis=0,
        tiled=True,
    ).reshape(seq_count, positions, q_width + k_width)
    query_back = jnp.concatenate([back[j, :, :q_width] for j in range(seq_count)], axis=1)
    key_back = jnp.concatenate([back[j, :, q_width:] for j in range(seq_count)], axis=1)
    mirror_value = lax.ppermute(value_out, "section", mirror)
    paired = weight_grads(own_gathered, mirror_gathered, value_out, mirror_value)
    return (query_back[None], key_back[None], paired[None])


def solution(mesh):
    in_specs = (
        P("section", "seq", None),
        P("section", "seq", None),
        P("section", "seq", None),
        P("section", "seq", None),
        P("section", "seq", None),
        P("section", "seq"),
    )
    out_specs = (P("section", "seq", None), P("section", "seq", None), P("section", None, "seq"))
    return jax.shard_map(local, mesh=mesh, in_specs=in_specs, out_specs=out_specs, check_vma=False)
```

```python
import math

import jax
import jax.numpy as jnp
from jax import lax
from jax.experimental import pallas as pl
from jax.experimental.pallas import tpu as pltpu
from jax.sharding import PartitionSpec as P

HEAD_WIDTH = 128


def attention_kernel(query_ref, key_ref, value_ref, grad_ref, doc_col_ref, doc_row_ref,
                     query_out_ref, key_out_ref, value_out_ref):
    head, tile = pl.program_id(1), pl.program_id(2)
    rows, length = query_ref.shape[0], key_ref.shape[0]
    scale_factor = 1.0 / math.sqrt(key_ref.shape[1])

    @pl.when((head == 0) & (tile == 0))
    def _():
        key_out_ref[...] = jnp.zeros(key_out_ref.shape, jnp.float32)
        value_out_ref[...] = jnp.zeros(value_out_ref.shape, jnp.float32)

    query_one, grad_one = query_ref[...], grad_ref[...]
    key_col, value_col = key_ref[...], value_ref[...]
    row_pos = tile * rows + lax.broadcasted_iota(jnp.int32, (rows, length), 0)
    col_pos = lax.broadcasted_iota(jnp.int32, (rows, length), 1)
    allowed = (row_pos >= col_pos) & (doc_col_ref[...] == doc_row_ref[...])
    contract_last = (((1,), (1,)), ((), ()))
    contract_first = (((0,), (0,)), ((), ()))
    scores = lax.dot_general(query_one, key_col, contract_last,
                             preferred_element_type=jnp.float32) * scale_factor
    scores = jnp.where(allowed, scores, -jnp.inf)
    row_max = jnp.max(scores, axis=1, keepdims=True)
    weights = jnp.exp(scores - row_max)
    attention = weights / jnp.sum(weights, axis=1, keepdims=True)
    probs_low = attention.astype(jnp.bfloat16)
    attended = jnp.dot(probs_low, value_col, preferred_element_type=jnp.float32).astype(jnp.bfloat16)
    row_delta = jnp.sum(grad_one.astype(jnp.float32) * attended.astype(jnp.float32),
                        axis=1, keepdims=True)
    dprobs = lax.dot_general(grad_one, value_col, contract_last,
                             preferred_element_type=jnp.float32)
    dscores = (attention * (dprobs - row_delta) * scale_factor).astype(jnp.bfloat16)
    query_out_ref[...] = jnp.dot(dscores, key_col,
                                 preferred_element_type=jnp.float32).astype(jnp.bfloat16)
    key_out_ref[...] += lax.dot_general(dscores, query_one, contract_first,
                                        preferred_element_type=jnp.float32)
    value_out_ref[...] += lax.dot_general(probs_low, grad_one, contract_first,
                                          preferred_element_type=jnp.float32)


def attention_grads(merged, doc_ids, q_width, k_width):
    length = merged.shape[0]
    kv_heads = k_width // HEAD_WIDTH
    group_size = q_width // k_width
    rows = min(length, 256)
    tiles = length // rows
    q_blocks, k_blocks = q_width // HEAD_WIDTH, k_width // HEAD_WIDTH

    def head_at(base):
        return pl.BlockSpec((rows, HEAD_WIDTH), lambda g, h, t: (t, base + g * group_size + h))

    def kv_at(base):
        return pl.BlockSpec((length, HEAD_WIDTH), lambda g, h, t: (0, base + g))

    query_out, key_acc, value_acc = pl.pallas_call(
        attention_kernel,
        grid=(kv_heads, group_size, tiles),
        in_specs=[
            head_at(0),
            kv_at(2 * q_blocks),
            kv_at(2 * q_blocks + k_blocks),
            head_at(q_blocks),
            pl.BlockSpec((rows, 1), lambda g, h, t: (t, 0)),
            pl.BlockSpec((1, length), lambda g, h, t: (0, 0)),
        ],
        out_specs=[
            pl.BlockSpec((rows, HEAD_WIDTH), lambda g, h, t: (t, g * group_size + h)),
            kv_at(0),
            kv_at(0),
        ],
        out_shape=[
            jax.ShapeDtypeStruct((length, q_width), jnp.bfloat16),
            jax.ShapeDtypeStruct((length, k_width), jnp.float32),
            jax.ShapeDtypeStruct((length, k_width), jnp.float32),
        ],
        compiler_params=pltpu.CompilerParams(
            dimension_semantics=("arbitrary", "arbitrary", "arbitrary"),
            vmem_limit_bytes=48 * 1024 * 1024,
        ),
    )(merged, merged, merged, merged, doc_ids.reshape(length, 1), doc_ids.reshape(1, length))
    return (query_out, key_acc.astype(jnp.bfloat16), value_acc.astype(jnp.bfloat16))


def weight_kernel(own_ref, mirror_ref, own_value_ref, mirror_value_ref, *refs):
    out_ref = refs[-1]
    contract_first = (((0,), (0,)), ((), ()))
    total = lax.dot_general(own_ref[...], own_value_ref[...], contract_first,
                            preferred_element_type=jnp.float32)
    total = total + lax.dot_general(mirror_ref[...], mirror_value_ref[...], contract_first,
                                    preferred_element_type=jnp.float32)
    out_ref[...] = total.astype(out_ref.dtype)


def weight_range(own_rows, mirror_rows, own_values, mirror_values, first, prior=None):
    positions, width = own_rows.shape
    cols = own_values.shape[1]
    tile = 512
    base = first // tile
    count = mirror_rows.shape[1] // tile
    in_specs = [
        pl.BlockSpec((positions, tile), lambda i: (0, base + i)),
        pl.BlockSpec((positions, tile), lambda i: (0, i)),
        pl.BlockSpec((positions, cols), lambda i: (0, 0)),
        pl.BlockSpec((positions, cols), lambda i: (0, 0)),
    ]
    operands = [own_rows, mirror_rows, own_values, mirror_values]
    aliases = {}
    if prior is not None:
        in_specs.append(pl.BlockSpec(memory_space=pl.ANY))
        operands.append(prior)
        aliases = {4: 0}
    return pl.pallas_call(
        weight_kernel,
        grid=(count,),
        in_specs=in_specs,
        out_specs=pl.BlockSpec((tile, cols), lambda i: (base + i, 0)),
        out_shape=jax.ShapeDtypeStruct((width, cols), jnp.bfloat16),
        input_output_aliases=aliases,
        compiler_params=pltpu.CompilerParams(dimension_semantics=("arbitrary",)),
    )(*operands)


def local(queries, key_states, section_value_states, out_grad, layer_input, doc_segments):
    section_count = lax.axis_size("section")
    seq_count = lax.axis_size("seq")
    seq_index = lax.axis_index("seq")
    mirror = [(i, section_count - 1 - i) for i in range(section_count)]
    own_rows = layer_input[0]
    own_gathered = lax.all_gather(own_rows, "seq", axis=0, tiled=True)
    mirror_rows = lax.ppermute(own_rows, "section", mirror)
    positions = queries.shape[1]
    q_width = queries.shape[2] // seq_count
    k_width = key_states.shape[2] // seq_count
    parts = [
        queries[0].reshape(positions, seq_count, q_width),
        out_grad[0].reshape(positions, seq_count, q_width),
        key_states[0].reshape(positions, seq_count, k_width),
        section_value_states[0].reshape(positions, seq_count, k_width),
    ]
    merged = lax.all_to_all(
        jnp.concatenate(parts, axis=2), "seq", split_axis=1, concat_axis=0, tiled=True
    ).reshape(positions * seq_count, 2 * q_width + 2 * k_width)
    doc_ids = lax.all_to_all(
        jnp.broadcast_to(doc_segments, (seq_count, positions)), "seq",
        split_axis=0, concat_axis=0, tiled=True,
    ).reshape(seq_count * positions)
    merged, mirror_rows = lax.optimization_barrier((merged, mirror_rows))
    width = mirror_rows.shape[1]
    split = (width // 8) * 5
    mirror_near = lax.all_gather(mirror_rows[:, :split], "seq", axis=0, tiled=True)
    far_rows = mirror_rows[:, split:]
    mirror_far = lax.all_to_all(
        jnp.broadcast_to(far_rows, (seq_count,) + far_rows.shape), "seq",
        split_axis=0, concat_axis=0, tiled=True,
    ).reshape(seq_count * far_rows.shape[0], far_rows.shape[1])
    query_out, key_out, value_out = attention_grads(merged, doc_ids, q_width, k_width)
    back = lax.all_to_all(
        jnp.concatenate([query_out, key_out], axis=1), "seq", split_axis=0, concat_axis=0,
        tiled=True,
    ).reshape(seq_count, positions, q_width + k_width)
    query_back = jnp.concatenate([back[j, :, :q_width] for j in range(seq_count)], axis=1)
    key_back = jnp.concatenate([back[j, :, q_width:] for j in range(seq_count)], axis=1)
    mirror_value = lax.ppermute(value_out, "section", mirror)
    paired = weight_range(own_gathered, mirror_near, value_out, mirror_value, 0)
    paired = weight_range(own_gathered, mirror_far, value_out, mirror_value, split, paired)
    return (query_back[None], key_back[None], paired[None])


def solution(mesh):
    in_specs = (
        P("section", "seq", None),
        P("section", "seq", None),
        P("section", "seq", None),
        P("section", "seq", None),
        P("section", "seq", None),
        P("section", "seq"),
    )
    out_specs = (P("section", "seq", None), P("section", "seq", None), P("section", None, "seq"))
    return jax.shard_map(local, mesh=mesh, in_specs=in_specs, out_specs=out_specs, check_vma=False)
```

```python
import math

import jax
import jax.numpy as jnp
from jax import lax
from jax.experimental import pallas as pl
from jax.experimental.pallas import tpu as pltpu
from jax.sharding import PartitionSpec as P

HEAD_WIDTH = 128


def attention_kernel(query_ref, key_ref, value_ref, grad_ref, doc_col_ref, doc_row_ref,
                     query_out_ref, key_out_ref, value_out_ref):
    head, tile = pl.program_id(1), pl.program_id(2)
    rows, length = query_ref.shape[0], key_ref.shape[0]
    scale_factor = 1.0 / math.sqrt(key_ref.shape[1])

    @pl.when((head == 0) & (tile == 0))
    def _():
        key_out_ref[...] = jnp.zeros(key_out_ref.shape, jnp.float32)
        value_out_ref[...] = jnp.zeros(value_out_ref.shape, jnp.float32)

    query_one, grad_one = query_ref[...], grad_ref[...]
    key_col, value_col = key_ref[...], value_ref[...]
    row_pos = tile * rows + lax.broadcasted_iota(jnp.int32, (rows, length), 0)
    col_pos = lax.broadcasted_iota(jnp.int32, (rows, length), 1)
    allowed = (row_pos >= col_pos) & (doc_col_ref[...] == doc_row_ref[...])
    contract_last = (((1,), (1,)), ((), ()))
    contract_first = (((0,), (0,)), ((), ()))
    scores = lax.dot_general(query_one, key_col, contract_last,
                             preferred_element_type=jnp.float32) * scale_factor
    scores = jnp.where(allowed, scores, -jnp.inf)
    row_max = jnp.max(scores, axis=1, keepdims=True)
    weights = jnp.exp(scores - row_max)
    attention = weights / jnp.sum(weights, axis=1, keepdims=True)
    probs_low = attention.astype(jnp.bfloat16)
    attended = jnp.dot(probs_low, value_col, preferred_element_type=jnp.float32).astype(jnp.bfloat16)
    row_delta = jnp.sum(grad_one.astype(jnp.float32) * attended.astype(jnp.float32),
                        axis=1, keepdims=True)
    dprobs = lax.dot_general(grad_one, value_col, contract_last,
                             preferred_element_type=jnp.float32)
    dscores = (attention * (dprobs - row_delta) * scale_factor).astype(jnp.bfloat16)
    query_out_ref[...] = jnp.dot(dscores, key_col,
                                 preferred_element_type=jnp.float32).astype(jnp.bfloat16)
    key_out_ref[...] += lax.dot_general(dscores, query_one, contract_first,
                                        preferred_element_type=jnp.float32)
    value_out_ref[...] += lax.dot_general(probs_low, grad_one, contract_first,
                                          preferred_element_type=jnp.float32)


def attention_grads(merged, doc_ids, q_width, k_width):
    length = merged.shape[0]
    kv_heads = k_width // HEAD_WIDTH
    group_size = q_width // k_width
    rows = min(length, 256)
    tiles = length // rows
    q_blocks, k_blocks = q_width // HEAD_WIDTH, k_width // HEAD_WIDTH

    def head_at(base):
        return pl.BlockSpec((rows, HEAD_WIDTH), lambda g, h, t: (t, base + g * group_size + h))

    def kv_at(base):
        return pl.BlockSpec((length, HEAD_WIDTH), lambda g, h, t: (0, base + g))

    query_out, key_acc, value_acc = pl.pallas_call(
        attention_kernel,
        grid=(kv_heads, group_size, tiles),
        in_specs=[
            head_at(0),
            kv_at(2 * q_blocks),
            kv_at(2 * q_blocks + k_blocks),
            head_at(q_blocks),
            pl.BlockSpec((rows, 1), lambda g, h, t: (t, 0)),
            pl.BlockSpec((1, length), lambda g, h, t: (0, 0)),
        ],
        out_specs=[
            pl.BlockSpec((rows, HEAD_WIDTH), lambda g, h, t: (t, g * group_size + h)),
            kv_at(0),
            kv_at(0),
        ],
        out_shape=[
            jax.ShapeDtypeStruct((length, q_width), jnp.bfloat16),
            jax.ShapeDtypeStruct((length, k_width), jnp.float32),
            jax.ShapeDtypeStruct((length, k_width), jnp.float32),
        ],
        compiler_params=pltpu.CompilerParams(
            dimension_semantics=("arbitrary", "arbitrary", "arbitrary"),
            vmem_limit_bytes=48 * 1024 * 1024,
        ),
    )(merged, merged, merged, merged, doc_ids.reshape(length, 1), doc_ids.reshape(1, length))
    return (query_out, key_acc.astype(jnp.bfloat16), value_acc.astype(jnp.bfloat16))


def weight_kernel(own_ref, mirror_ref, own_value_ref, mirror_value_ref, out_ref):
    contract_first = (((0,), (0,)), ((), ()))
    total = lax.dot_general(own_ref[...], own_value_ref[...], contract_first,
                            preferred_element_type=jnp.float32)
    total = total + lax.dot_general(mirror_ref[...], mirror_value_ref[...], contract_first,
                                    preferred_element_type=jnp.float32)
    out_ref[...] = total.astype(out_ref.dtype)


def weight_grads(own_rows, mirror_rows, own_values, mirror_values):
    positions, width = own_rows.shape
    cols = own_values.shape[1]
    tile = min(width, 2048)
    row_spec = pl.BlockSpec((positions, tile), lambda i: (0, i))
    value_spec = pl.BlockSpec((positions, cols), lambda i: (0, 0))
    return pl.pallas_call(
        weight_kernel,
        grid=(width // tile,),
        in_specs=[row_spec, row_spec, value_spec, value_spec],
        out_specs=pl.BlockSpec((tile, cols), lambda i: (i, 0)),
        out_shape=jax.ShapeDtypeStruct((width, cols), jnp.bfloat16),
        compiler_params=pltpu.CompilerParams(
            dimension_semantics=("arbitrary",), vmem_limit_bytes=48 * 1024 * 1024
        ),
    )(own_rows, mirror_rows, own_values, mirror_values)


def local(queries, key_states, section_value_states, out_grad, layer_input, doc_segments):
    section_count = lax.axis_size("section")
    seq_count = lax.axis_size("seq")
    seq_index = lax.axis_index("seq")
    mirror = [(i, section_count - 1 - i) for i in range(section_count)]
    own_rows = layer_input[0]
    own_gathered = lax.all_gather(own_rows, "seq", axis=0, tiled=True)
    mirror_rows = lax.ppermute(own_rows, "section", mirror)
    positions = queries.shape[1]
    q_width = queries.shape[2] // seq_count
    k_width = key_states.shape[2] // seq_count
    parts = [
        queries[0].reshape(positions, seq_count, q_width),
        out_grad[0].reshape(positions, seq_count, q_width),
        key_states[0].reshape(positions, seq_count, k_width),
        section_value_states[0].reshape(positions, seq_count, k_width),
    ]
    merged = lax.all_to_all(
        jnp.concatenate(parts, axis=2), "seq", split_axis=1, concat_axis=0, tiled=True
    ).reshape(positions * seq_count, 2 * q_width + 2 * k_width)
    doc_ids = lax.all_to_all(
        jnp.broadcast_to(doc_segments, (seq_count, positions)), "seq",
        split_axis=0, concat_axis=0, tiled=True,
    ).reshape(seq_count * positions)
    merged, mirror_rows = lax.optimization_barrier((merged, mirror_rows))
    mirror_gathered = lax.all_gather(mirror_rows, "seq", axis=0, tiled=True)
    query_out, key_out, value_out = attention_grads(merged, doc_ids, q_width, k_width)
    back = lax.all_to_all(
        jnp.concatenate([query_out, key_out], axis=1), "seq", split_axis=0, concat_axis=0,
        tiled=True,
    ).reshape(seq_count, positions, q_width + k_width)
    query_back = jnp.concatenate([back[j, :, :q_width] for j in range(seq_count)], axis=1)
    key_back = jnp.concatenate([back[j, :, q_width:] for j in range(seq_count)], axis=1)
    mirror_value = lax.ppermute(value_out, "section", mirror)
    paired = weight_grads(own_gathered, mirror_gathered, value_out, mirror_value)
    return (query_back[None], key_back[None], paired[None])


def solution(mesh):
    in_specs = (
        P("section", "seq", None),
        P("section", "seq", None),
        P("section", "seq", None),
        P("section", "seq", None),
        P("section", "seq", None),
        P("section", "seq"),
    )
    out_specs = (P("section", "seq", None), P("section", "seq", None), P("section", None, "seq"))
    return jax.shard_map(local, mesh=mesh, in_specs=in_specs, out_specs=out_specs, check_vma=False)
```

```python
import math

import jax
import jax.numpy as jnp
from jax import lax
from jax.experimental import pallas as pl
from jax.experimental.pallas import tpu as pltpu
from jax.sharding import PartitionSpec as P

HEAD_WIDTH = 128


def attention_kernel(query_ref, key_ref, value_ref, grad_ref, doc_col_ref, doc_row_ref,
                     query_out_ref, key_out_ref, value_out_ref):
    head, tile = pl.program_id(1), pl.program_id(2)
    rows, length = query_ref.shape[0], key_ref.shape[0]
    scale_factor = 1.0 / math.sqrt(key_ref.shape[1])

    @pl.when((head == 0) & (tile == 0))
    def _():
        key_out_ref[...] = jnp.zeros(key_out_ref.shape, jnp.float32)
        value_out_ref[...] = jnp.zeros(value_out_ref.shape, jnp.float32)

    query_one, grad_one = query_ref[...], grad_ref[...]
    key_col, value_col = key_ref[...], value_ref[...]
    row_pos = tile * rows + lax.broadcasted_iota(jnp.int32, (rows, length), 0)
    col_pos = lax.broadcasted_iota(jnp.int32, (rows, length), 1)
    allowed = (row_pos >= col_pos) & (doc_col_ref[...] == doc_row_ref[...])
    contract_last = (((1,), (1,)), ((), ()))
    contract_first = (((0,), (0,)), ((), ()))
    scores = lax.dot_general(query_one, key_col, contract_last,
                             preferred_element_type=jnp.float32) * scale_factor
    scores = jnp.where(allowed, scores, -jnp.inf)
    row_max = jnp.max(scores, axis=1, keepdims=True)
    weights = jnp.exp(scores - row_max)
    attention = weights / jnp.sum(weights, axis=1, keepdims=True)
    probs_low = attention.astype(jnp.bfloat16)
    attended = jnp.dot(probs_low, value_col, preferred_element_type=jnp.float32).astype(jnp.bfloat16)
    row_delta = jnp.sum(grad_one.astype(jnp.float32) * attended.astype(jnp.float32),
                        axis=1, keepdims=True)
    dprobs = lax.dot_general(grad_one, value_col, contract_last,
                             preferred_element_type=jnp.float32)
    dscores = (attention * (dprobs - row_delta) * scale_factor).astype(jnp.bfloat16)
    query_out_ref[...] = jnp.dot(dscores, key_col,
                                 preferred_element_type=jnp.float32).astype(jnp.bfloat16)
    key_out_ref[...] += lax.dot_general(dscores, query_one, contract_first,
                                        preferred_element_type=jnp.float32)
    value_out_ref[...] += lax.dot_general(probs_low, grad_one, contract_first,
                                          preferred_element_type=jnp.float32)


def attention_grads(merged, doc_ids, q_width, k_width):
    length = merged.shape[0]
    kv_heads = k_width // HEAD_WIDTH
    group_size = q_width // k_width
    rows = min(length, 256)
    tiles = length // rows
    q_blocks, k_blocks = q_width // HEAD_WIDTH, k_width // HEAD_WIDTH

    def head_at(base):
        return pl.BlockSpec((rows, HEAD_WIDTH), lambda g, h, t: (t, base + g * group_size + h))

    def kv_at(base):
        return pl.BlockSpec((length, HEAD_WIDTH), lambda g, h, t: (0, base + g))

    query_out, key_acc, value_acc = pl.pallas_call(
        attention_kernel,
        grid=(kv_heads, group_size, tiles),
        in_specs=[
            head_at(0),
            kv_at(2 * q_blocks),
            kv_at(2 * q_blocks + k_blocks),
            head_at(q_blocks),
            pl.BlockSpec((rows, 1), lambda g, h, t: (t, 0)),
            pl.BlockSpec((1, length), lambda g, h, t: (0, 0)),
        ],
        out_specs=[
            pl.BlockSpec((rows, HEAD_WIDTH), lambda g, h, t: (t, g * group_size + h)),
            kv_at(0),
            kv_at(0),
        ],
        out_shape=[
            jax.ShapeDtypeStruct((length, q_width), jnp.bfloat16),
            jax.ShapeDtypeStruct((length, k_width), jnp.float32),
            jax.ShapeDtypeStruct((length, k_width), jnp.float32),
        ],
        compiler_params=pltpu.CompilerParams(
            dimension_semantics=("arbitrary", "arbitrary", "arbitrary"),
            vmem_limit_bytes=48 * 1024 * 1024,
        ),
    )(merged, merged, merged, merged, doc_ids.reshape(length, 1), doc_ids.reshape(1, length))
    return (query_out, key_acc.astype(jnp.bfloat16), value_acc.astype(jnp.bfloat16))


def weight_kernel(own_ref, mirror_ref, own_value_ref, mirror_value_ref, *refs):
    out_ref = refs[-1]
    contract_first = (((0,), (0,)), ((), ()))
    total = lax.dot_general(own_ref[...], own_value_ref[...], contract_first,
                            preferred_element_type=jnp.float32)
    total = total + lax.dot_general(mirror_ref[...], mirror_value_ref[...], contract_first,
                                    preferred_element_type=jnp.float32)
    out_ref[...] = total.astype(out_ref.dtype)


def weight_range(own_rows, own_base, mirror_rows, mirror_base, own_values, mirror_values,
                 out_base, count, tile, width, prior=None):
    positions = own_rows.shape[0]
    cols = own_values.shape[1]
    in_specs = [
        pl.BlockSpec((positions, tile), lambda i: (0, own_base + i)),
        pl.BlockSpec((positions, tile), lambda i: (0, mirror_base + i)),
        pl.BlockSpec((positions, cols), lambda i: (0, 0)),
        pl.BlockSpec((positions, cols), lambda i: (0, 0)),
    ]
    operands = [own_rows, mirror_rows, own_values, mirror_values]
    aliases = {}
    if prior is not None:
        in_specs.append(pl.BlockSpec(memory_space=pl.ANY))
        operands.append(prior)
        aliases = {4: 0}
    return pl.pallas_call(
        weight_kernel,
        grid=(count,),
        in_specs=in_specs,
        out_specs=pl.BlockSpec((tile, cols), lambda i: (out_base + i, 0)),
        out_shape=jax.ShapeDtypeStruct((width, cols), jnp.bfloat16),
        input_output_aliases=aliases,
        compiler_params=pltpu.CompilerParams(
            dimension_semantics=("arbitrary",), vmem_limit_bytes=48 * 1024 * 1024
        ),
    )(*operands)


def local(queries, key_states, section_value_states, out_grad, layer_input, doc_segments):
    section_count = lax.axis_size("section")
    seq_count = lax.axis_size("seq")
    seq_index = lax.axis_index("seq")
    mirror = [(i, section_count - 1 - i) for i in range(section_count)]
    own_rows = layer_input[0]
    width = own_rows.shape[1]
    near = width - width // 4
    own_gathered = lax.all_gather(own_rows[:, :near], "seq", axis=0, tiled=True)
    mirror_rows = lax.ppermute(own_rows, "section", mirror)
    positions = queries.shape[1]
    q_width = queries.shape[2] // seq_count
    k_width = key_states.shape[2] // seq_count
    parts = [
        queries[0].reshape(positions, seq_count, q_width),
        out_grad[0].reshape(positions, seq_count, q_width),
        key_states[0].reshape(positions, seq_count, k_width),
        section_value_states[0].reshape(positions, seq_count, k_width),
        jnp.broadcast_to(own_rows[:, None, near:], (positions, seq_count, width - near)),
    ]
    merged = lax.all_to_all(
        jnp.concatenate(parts, axis=2), "seq", split_axis=1, concat_axis=0, tiled=True
    ).reshape(positions * seq_count, 2 * q_width + 2 * k_width + width - near)
    doc_ids = lax.all_to_all(
        jnp.broadcast_to(doc_segments, (seq_count, positions)), "seq",
        split_axis=0, concat_axis=0, tiled=True,
    ).reshape(seq_count * positions)
    merged, mirror_rows = lax.optimization_barrier((merged, mirror_rows))
    mirror_gathered = lax.all_gather(mirror_rows, "seq", axis=0, tiled=True)
    query_out, key_out, value_out = attention_grads(merged, doc_ids, q_width, k_width)
    back = lax.all_to_all(
        jnp.concatenate([query_out, key_out], axis=1), "seq", split_axis=0, concat_axis=0,
        tiled=True,
    ).reshape(seq_count, positions, q_width + k_width)
    query_back = jnp.concatenate([back[j, :, :q_width] for j in range(seq_count)], axis=1)
    key_back = jnp.concatenate([back[j, :, q_width:] for j in range(seq_count)], axis=1)
    mirror_value = lax.ppermute(value_out, "section", mirror)
    big, small = min(width, 2048), 512
    while (2 * q_width + 2 * k_width) % small or near % small:
        small //= 2
    paired = weight_range(own_gathered, 0, mirror_gathered, 0, value_out, mirror_value,
                          0, near // big, big, width)
    merged_base = (2 * q_width + 2 * k_width) // small
    paired = weight_range(merged, merged_base, mirror_gathered, near // small, value_out,
                          mirror_value, near // small, (width - near) // small, small, width,
                          paired)
    return (query_back[None], key_back[None], paired[None])


def solution(mesh):
    in_specs = (
        P("section", "seq", None),
        P("section", "seq", None),
        P("section", "seq", None),
        P("section", "seq", None),
        P("section", "seq", None),
        P("section", "seq"),
    )
    out_specs = (P("section", "seq", None), P("section", "seq", None), P("section", None, "seq"))
    return jax.shard_map(local, mesh=mesh, in_specs=in_specs, out_specs=out_specs, check_vma=False)
```

```python
import math

import jax
import jax.numpy as jnp
from jax import lax
from jax.experimental import pallas as pl
from jax.experimental.pallas import tpu as pltpu
from jax.sharding import PartitionSpec as P

HEAD_WIDTH = 128


def attention_kernel(query_ref, key_ref, value_ref, grad_ref, doc_col_ref, doc_row_ref,
                     query_out_ref, key_out_ref, value_out_ref):
    head, tile = pl.program_id(1), pl.program_id(2)
    rows, length = query_ref.shape[0], key_ref.shape[0]
    scale_factor = 1.0 / math.sqrt(key_ref.shape[1])

    @pl.when((head == 0) & (tile == 0))
    def _():
        key_out_ref[...] = jnp.zeros(key_out_ref.shape, jnp.float32)
        value_out_ref[...] = jnp.zeros(value_out_ref.shape, jnp.float32)

    query_one, grad_one = query_ref[...], grad_ref[...]
    key_col, value_col = key_ref[...], value_ref[...]
    row_pos = tile * rows + lax.broadcasted_iota(jnp.int32, (rows, length), 0)
    col_pos = lax.broadcasted_iota(jnp.int32, (rows, length), 1)
    allowed = (row_pos >= col_pos) & (doc_col_ref[...] == doc_row_ref[...])
    contract_last = (((1,), (1,)), ((), ()))
    contract_first = (((0,), (0,)), ((), ()))
    scores = lax.dot_general(query_one, key_col, contract_last,
                             preferred_element_type=jnp.float32) * scale_factor
    scores = jnp.where(allowed, scores, -jnp.inf)
    row_max = jnp.max(scores, axis=1, keepdims=True)
    weights = jnp.exp(scores - row_max)
    attention = weights / jnp.sum(weights, axis=1, keepdims=True)
    probs_low = attention.astype(jnp.bfloat16)
    attended = jnp.dot(probs_low, value_col, preferred_element_type=jnp.float32).astype(jnp.bfloat16)
    row_delta = jnp.sum(grad_one.astype(jnp.float32) * attended.astype(jnp.float32),
                        axis=1, keepdims=True)
    dprobs = lax.dot_general(grad_one, value_col, contract_last,
                             preferred_element_type=jnp.float32)
    dscores = (attention * (dprobs - row_delta) * scale_factor).astype(jnp.bfloat16)
    query_out_ref[...] = jnp.dot(dscores, key_col,
                                 preferred_element_type=jnp.float32).astype(jnp.bfloat16)
    key_out_ref[...] += lax.dot_general(dscores, query_one, contract_first,
                                        preferred_element_type=jnp.float32)
    value_out_ref[...] += lax.dot_general(probs_low, grad_one, contract_first,
                                          preferred_element_type=jnp.float32)


def attention_grads(merged, doc_ids, q_width, k_width):
    length = merged.shape[0]
    kv_heads = k_width // HEAD_WIDTH
    group_size = q_width // k_width
    rows = min(length, 256)
    tiles = length // rows
    q_blocks, k_blocks = q_width // HEAD_WIDTH, k_width // HEAD_WIDTH

    def head_at(base):
        return pl.BlockSpec((rows, HEAD_WIDTH), lambda g, h, t: (t, base + g * group_size + h))

    def kv_at(base):
        return pl.BlockSpec((length, HEAD_WIDTH), lambda g, h, t: (0, base + g))

    query_out, key_acc, value_acc = pl.pallas_call(
        attention_kernel,
        grid=(kv_heads, group_size, tiles),
        in_specs=[
            head_at(0),
            kv_at(2 * q_blocks),
            kv_at(2 * q_blocks + k_blocks),
            head_at(q_blocks),
            pl.BlockSpec((rows, 1), lambda g, h, t: (t, 0)),
            pl.BlockSpec((1, length), lambda g, h, t: (0, 0)),
        ],
        out_specs=[
            pl.BlockSpec((rows, HEAD_WIDTH), lambda g, h, t: (t, g * group_size + h)),
            kv_at(0),
            kv_at(0),
        ],
        out_shape=[
            jax.ShapeDtypeStruct((length, q_width), jnp.bfloat16),
            jax.ShapeDtypeStruct((length, k_width), jnp.float32),
            jax.ShapeDtypeStruct((length, k_width), jnp.float32),
        ],
        compiler_params=pltpu.CompilerParams(
            dimension_semantics=("arbitrary", "arbitrary", "arbitrary"),
            vmem_limit_bytes=48 * 1024 * 1024,
        ),
    )(merged, merged, merged, merged, doc_ids.reshape(length, 1), doc_ids.reshape(1, length))
    return (query_out, key_acc.astype(jnp.bfloat16), value_acc.astype(jnp.bfloat16))


def weight_kernel(own_ref, mirror_ref, own_value_ref, mirror_value_ref, *refs):
    out_ref = refs[-1]
    contract_first = (((0,), (0,)), ((), ()))
    total = lax.dot_general(own_ref[...], own_value_ref[...], contract_first,
                            preferred_element_type=jnp.float32)
    total = total + lax.dot_general(mirror_ref[...], mirror_value_ref[...], contract_first,
                                    preferred_element_type=jnp.float32)
    out_ref[...] = total.astype(out_ref.dtype)


def weight_range(own_rows, own_base, mirror_rows, mirror_base, own_values, mirror_values,
                 out_base, count, tile, width, prior=None):
    positions = own_rows.shape[0]
    cols = own_values.shape[1]
    in_specs = [
        pl.BlockSpec((positions, tile), lambda i: (0, own_base + i)),
        pl.BlockSpec((positions, tile), lambda i: (0, mirror_base + i)),
        pl.BlockSpec((positions, cols), lambda i: (0, 0)),
        pl.BlockSpec((positions, cols), lambda i: (0, 0)),
    ]
    operands = [own_rows, mirror_rows, own_values, mirror_values]
    aliases = {}
    if prior is not None:
        in_specs.append(pl.BlockSpec(memory_space=pl.ANY))
        operands.append(prior)
        aliases = {4: 0}
    return pl.pallas_call(
        weight_kernel,
        grid=(count,),
        in_specs=in_specs,
        out_specs=pl.BlockSpec((tile, cols), lambda i: (out_base + i, 0)),
        out_shape=jax.ShapeDtypeStruct((width, cols), jnp.bfloat16),
        input_output_aliases=aliases,
        compiler_params=pltpu.CompilerParams(
            dimension_semantics=("arbitrary",), vmem_limit_bytes=48 * 1024 * 1024
        ),
    )(*operands)


def local(queries, key_states, section_value_states, out_grad, layer_input, doc_segments):
    section_count = lax.axis_size("section")
    seq_count = lax.axis_size("seq")
    seq_index = lax.axis_index("seq")
    mirror = [(i, section_count - 1 - i) for i in range(section_count)]
    own_rows = layer_input[0]
    width = own_rows.shape[1]
    near = width - width // 8
    own_gathered = lax.all_gather(own_rows[:, :near], "seq", axis=0, tiled=True)
    mirror_rows = lax.ppermute(own_rows, "section", mirror)
    positions = queries.shape[1]
    q_width = queries.shape[2] // seq_count
    k_width = key_states.shape[2] // seq_count
    parts = [
        queries[0].reshape(positions, seq_count, q_width),
        out_grad[0].reshape(positions, seq_count, q_width),
        key_states[0].reshape(positions, seq_count, k_width),
        section_value_states[0].reshape(positions, seq_count, k_width),
        jnp.broadcast_to(own_rows[:, None, near:], (positions, seq_count, width - near)),
    ]
    merged = lax.all_to_all(
        jnp.concatenate(parts, axis=2), "seq", split_axis=1, concat_axis=0, tiled=True
    ).reshape(positions * seq_count, 2 * q_width + 2 * k_width + width - near)
    doc_ids = lax.all_to_all(
        jnp.broadcast_to(doc_segments, (seq_count, positions)), "seq",
        split_axis=0, concat_axis=0, tiled=True,
    ).reshape(seq_count * positions)
    merged, mirror_rows = lax.optimization_barrier((merged, mirror_rows))
    mirror_gathered = lax.all_gather(mirror_rows, "seq", axis=0, tiled=True)
    query_out, key_out, value_out = attention_grads(merged, doc_ids, q_width, k_width)
    back = lax.all_to_all(
        jnp.concatenate([query_out, key_out], axis=1), "seq", split_axis=0, concat_axis=0,
        tiled=True,
    ).reshape(seq_count, positions, q_width + k_width)
    query_back = jnp.concatenate([back[j, :, :q_width] for j in range(seq_count)], axis=1)
    key_back = jnp.concatenate([back[j, :, q_width:] for j in range(seq_count)], axis=1)
    mirror_value = lax.ppermute(value_out, "section", mirror)
    big, small = min(width, 2048), 512
    while near % big:
        big //= 2
    while (2 * q_width + 2 * k_width) % small or near % small:
        small //= 2
    paired = weight_range(own_gathered, 0, mirror_gathered, 0, value_out, mirror_value,
                          0, near // big, big, width)
    merged_base = (2 * q_width + 2 * k_width) // small
    paired = weight_range(merged, merged_base, mirror_gathered, near // small, value_out,
                          mirror_value, near // small, (width - near) // small, small, width,
                          paired)
    return (query_back[None], key_back[None], paired[None])


def solution(mesh):
    in_specs = (
        P("section", "seq", None),
        P("section", "seq", None),
        P("section", "seq", None),
        P("section", "seq", None),
        P("section", "seq", None),
        P("section", "seq"),
    )
    out_specs = (P("section", "seq", None), P("section", "seq", None), P("section", None, "seq"))
    return jax.shard_map(local, mesh=mesh, in_specs=in_specs, out_specs=out_specs, check_vma=False)
```

```python
import math

import jax
import jax.numpy as jnp
from jax import lax
from jax.experimental import pallas as pl
from jax.experimental.pallas import tpu as pltpu
from jax.sharding import PartitionSpec as P

HEAD_WIDTH = 128


def attention_kernel(query_ref, key_ref, value_ref, grad_ref, doc_col_ref, doc_row_ref,
                     query_out_ref, key_out_ref, value_out_ref):
    head, tile = pl.program_id(1), pl.program_id(2)
    rows, length = query_ref.shape[0], key_ref.shape[0]
    scale_factor = 1.0 / math.sqrt(key_ref.shape[1])

    @pl.when((head == 0) & (tile == 0))
    def _():
        key_out_ref[...] = jnp.zeros(key_out_ref.shape, jnp.float32)
        value_out_ref[...] = jnp.zeros(value_out_ref.shape, jnp.float32)

    query_one, grad_one = query_ref[...], grad_ref[...]
    key_col, value_col = key_ref[...], value_ref[...]
    row_pos = tile * rows + lax.broadcasted_iota(jnp.int32, (rows, length), 0)
    col_pos = lax.broadcasted_iota(jnp.int32, (rows, length), 1)
    allowed = (row_pos >= col_pos) & (doc_col_ref[...] == doc_row_ref[...])
    contract_last = (((1,), (1,)), ((), ()))
    contract_first = (((0,), (0,)), ((), ()))
    scores = lax.dot_general(query_one, key_col, contract_last,
                             preferred_element_type=jnp.float32) * scale_factor
    scores = jnp.where(allowed, scores, -jnp.inf)
    row_max = jnp.max(scores, axis=1, keepdims=True)
    weights = jnp.exp(scores - row_max)
    attention = weights / jnp.sum(weights, axis=1, keepdims=True)
    probs_low = attention.astype(jnp.bfloat16)
    attended = jnp.dot(probs_low, value_col, preferred_element_type=jnp.float32).astype(jnp.bfloat16)
    row_delta = jnp.sum(grad_one.astype(jnp.float32) * attended.astype(jnp.float32),
                        axis=1, keepdims=True)
    dprobs = lax.dot_general(grad_one, value_col, contract_last,
                             preferred_element_type=jnp.float32)
    dscores = (attention * (dprobs - row_delta) * scale_factor).astype(jnp.bfloat16)
    query_out_ref[...] = jnp.dot(dscores, key_col,
                                 preferred_element_type=jnp.float32).astype(jnp.bfloat16)
    key_out_ref[...] += lax.dot_general(dscores, query_one, contract_first,
                                        preferred_element_type=jnp.float32)
    value_out_ref[...] += lax.dot_general(probs_low, grad_one, contract_first,
                                          preferred_element_type=jnp.float32)


def attention_grads(merged, doc_ids, q_width, k_width):
    length = merged.shape[0]
    kv_heads = k_width // HEAD_WIDTH
    group_size = q_width // k_width
    rows = min(length, 256)
    tiles = length // rows
    q_blocks, k_blocks = q_width // HEAD_WIDTH, k_width // HEAD_WIDTH

    def head_at(base):
        return pl.BlockSpec((rows, HEAD_WIDTH), lambda g, h, t: (t, base + g * group_size + h))

    def kv_at(base):
        return pl.BlockSpec((length, HEAD_WIDTH), lambda g, h, t: (0, base + g))

    query_out, key_acc, value_acc = pl.pallas_call(
        attention_kernel,
        grid=(kv_heads, group_size, tiles),
        in_specs=[
            head_at(0),
            kv_at(2 * q_blocks),
            kv_at(2 * q_blocks + k_blocks),
            head_at(q_blocks),
            pl.BlockSpec((rows, 1), lambda g, h, t: (t, 0)),
            pl.BlockSpec((1, length), lambda g, h, t: (0, 0)),
        ],
        out_specs=[
            pl.BlockSpec((rows, HEAD_WIDTH), lambda g, h, t: (t, g * group_size + h)),
            kv_at(0),
            kv_at(0),
        ],
        out_shape=[
            jax.ShapeDtypeStruct((length, q_width), jnp.bfloat16),
            jax.ShapeDtypeStruct((length, k_width), jnp.float32),
            jax.ShapeDtypeStruct((length, k_width), jnp.float32),
        ],
        compiler_params=pltpu.CompilerParams(
            dimension_semantics=("arbitrary", "arbitrary", "arbitrary"),
            vmem_limit_bytes=48 * 1024 * 1024,
        ),
    )(merged, merged, merged, merged, doc_ids.reshape(length, 1), doc_ids.reshape(1, length))
    return (query_out, key_acc.astype(jnp.bfloat16), value_acc.astype(jnp.bfloat16))


def weight_kernel(own_ref, mirror_ref, own_value_ref, mirror_value_ref, *refs):
    out_ref = refs[-1]
    contract_first = (((0,), (0,)), ((), ()))
    total = lax.dot_general(own_ref[...], own_value_ref[...], contract_first,
                            preferred_element_type=jnp.float32)
    total = total + lax.dot_general(mirror_ref[...], mirror_value_ref[...], contract_first,
                                    preferred_element_type=jnp.float32)
    out_ref[...] = total.astype(out_ref.dtype)


def weight_range(own_rows, mirror_rows, own_values, mirror_values, first, prior=None):
    positions, width = own_rows.shape
    cols = own_values.shape[1]
    tile = 1024
    base = first // tile
    count = mirror_rows.shape[1] // tile
    in_specs = [
        pl.BlockSpec((positions, tile), lambda i: (0, base + i)),
        pl.BlockSpec((positions, tile), lambda i: (0, i)),
        pl.BlockSpec((positions, cols), lambda i: (0, 0)),
        pl.BlockSpec((positions, cols), lambda i: (0, 0)),
    ]
    operands = [own_rows, mirror_rows, own_values, mirror_values]
    aliases = {}
    if prior is not None:
        in_specs.append(pl.BlockSpec(memory_space=pl.ANY))
        operands.append(prior)
        aliases = {4: 0}
    return pl.pallas_call(
        weight_kernel,
        grid=(count,),
        in_specs=in_specs,
        out_specs=pl.BlockSpec((tile, cols), lambda i: (base + i, 0)),
        out_shape=jax.ShapeDtypeStruct((width, cols), jnp.bfloat16),
        input_output_aliases=aliases,
        compiler_params=pltpu.CompilerParams(
            dimension_semantics=("arbitrary",), vmem_limit_bytes=48 * 1024 * 1024
        ),
    )(*operands)


def local(queries, key_states, section_value_states, out_grad, layer_input, doc_segments):
    section_count = lax.axis_size("section")
    seq_count = lax.axis_size("seq")
    seq_index = lax.axis_index("seq")
    mirror = [(i, section_count - 1 - i) for i in range(section_count)]
    own_rows = layer_input[0]
    own_gathered = lax.all_gather(own_rows, "seq", axis=0, tiled=True)
    mirror_rows = lax.ppermute(own_rows, "section", mirror)
    positions = queries.shape[1]
    q_width = queries.shape[2] // seq_count
    k_width = key_states.shape[2] // seq_count
    parts = [
        queries[0].reshape(positions, seq_count, q_width),
        out_grad[0].reshape(positions, seq_count, q_width),
        key_states[0].reshape(positions, seq_count, k_width),
        section_value_states[0].reshape(positions, seq_count, k_width),
    ]
    merged = lax.all_to_all(
        jnp.concatenate(parts, axis=2), "seq", split_axis=1, concat_axis=0, tiled=True
    ).reshape(positions * seq_count, 2 * q_width + 2 * k_width)
    doc_ids = lax.all_to_all(
        jnp.broadcast_to(doc_segments, (seq_count, positions)), "seq",
        split_axis=0, concat_axis=0, tiled=True,
    ).reshape(seq_count * positions)
    merged, mirror_rows = lax.optimization_barrier((merged, mirror_rows))
    width = mirror_rows.shape[1]
    split = width - width // 8
    mirror_near = lax.all_gather(mirror_rows[:, :split], "seq", axis=0, tiled=True)
    query_out, key_out, value_out = attention_grads(merged, doc_ids, q_width, k_width)
    far_rows = mirror_rows[:, split:]
    query_out, key_out, value_out, far_rows = lax.optimization_barrier(
        (query_out, key_out, value_out, far_rows)
    )
    mirror_far = lax.all_to_all(
        jnp.broadcast_to(far_rows, (seq_count,) + far_rows.shape), "seq",
        split_axis=0, concat_axis=0, tiled=True,
    ).reshape(seq_count * far_rows.shape[0], far_rows.shape[1])
    back = lax.all_to_all(
        jnp.concatenate([query_out, key_out], axis=1), "seq", split_axis=0, concat_axis=0,
        tiled=True,
    ).reshape(seq_count, positions, q_width + k_width)
    query_back = jnp.concatenate([back[j, :, :q_width] for j in range(seq_count)], axis=1)
    key_back = jnp.concatenate([back[j, :, q_width:] for j in range(seq_count)], axis=1)
    mirror_value = lax.ppermute(value_out, "section", mirror)
    paired = weight_range(own_gathered, mirror_near, value_out, mirror_value, 0)
    paired = weight_range(own_gathered, mirror_far, value_out, mirror_value, split, paired)
    return (query_back[None], key_back[None], paired[None])


def solution(mesh):
    in_specs = (
        P("section", "seq", None),
        P("section", "seq", None),
        P("section", "seq", None),
        P("section", "seq", None),
        P("section", "seq", None),
        P("section", "seq"),
    )
    out_specs = (P("section", "seq", None), P("section", "seq", None), P("section", None, "seq"))
    return jax.shard_map(local, mesh=mesh, in_specs=in_specs, out_specs=out_specs, check_vma=False)
```

```python
import math

import jax
import jax.numpy as jnp
from jax import lax
from jax.experimental import pallas as pl
from jax.experimental.pallas import tpu as pltpu
from jax.sharding import PartitionSpec as P

HEAD_WIDTH = 128


def attention_kernel(query_ref, key_ref, value_ref, grad_ref, doc_col_ref, doc_row_ref,
                     query_out_ref, key_out_ref, value_out_ref):
    head, tile = pl.program_id(1), pl.program_id(2)
    rows, length = query_ref.shape[0], key_ref.shape[0]
    scale_factor = 1.0 / math.sqrt(key_ref.shape[1])

    @pl.when((head == 0) & (tile == 0))
    def _():
        key_out_ref[...] = jnp.zeros(key_out_ref.shape, jnp.float32)
        value_out_ref[...] = jnp.zeros(value_out_ref.shape, jnp.float32)

    query_one, grad_one = query_ref[...], grad_ref[...]
    key_col, value_col = key_ref[...], value_ref[...]
    row_pos = tile * rows + lax.broadcasted_iota(jnp.int32, (rows, length), 0)
    col_pos = lax.broadcasted_iota(jnp.int32, (rows, length), 1)
    allowed = (row_pos >= col_pos) & (doc_col_ref[...] == doc_row_ref[...])
    contract_last = (((1,), (1,)), ((), ()))
    contract_first = (((0,), (0,)), ((), ()))
    scores = lax.dot_general(query_one, key_col, contract_last,
                             preferred_element_type=jnp.float32) * scale_factor
    scores = jnp.where(allowed, scores, -jnp.inf)
    row_max = jnp.max(scores, axis=1, keepdims=True)
    weights = jnp.exp(scores - row_max)
    attention = weights / jnp.sum(weights, axis=1, keepdims=True)
    probs_low = attention.astype(jnp.bfloat16)
    attended = jnp.dot(probs_low, value_col, preferred_element_type=jnp.float32).astype(jnp.bfloat16)
    row_delta = jnp.sum(grad_one.astype(jnp.float32) * attended.astype(jnp.float32),
                        axis=1, keepdims=True)
    dprobs = lax.dot_general(grad_one, value_col, contract_last,
                             preferred_element_type=jnp.float32)
    dscores = (attention * (dprobs - row_delta) * scale_factor).astype(jnp.bfloat16)
    query_out_ref[...] = jnp.dot(dscores, key_col,
                                 preferred_element_type=jnp.float32).astype(jnp.bfloat16)
    key_out_ref[...] += lax.dot_general(dscores, query_one, contract_first,
                                        preferred_element_type=jnp.float32)
    value_out_ref[...] += lax.dot_general(probs_low, grad_one, contract_first,
                                          preferred_element_type=jnp.float32)


def attention_grads(merged, doc_ids, q_width, k_width):
    length = merged.shape[0]
    kv_heads = k_width // HEAD_WIDTH
    group_size = q_width // k_width
    rows = min(length, 256)
    tiles = length // rows
    q_blocks, k_blocks = q_width // HEAD_WIDTH, k_width // HEAD_WIDTH

    def head_at(base):
        return pl.BlockSpec((rows, HEAD_WIDTH), lambda g, h, t: (t, base + g * group_size + h))

    def kv_at(base):
        return pl.BlockSpec((length, HEAD_WIDTH), lambda g, h, t: (0, base + g))

    query_out, key_acc, value_acc = pl.pallas_call(
        attention_kernel,
        grid=(kv_heads, group_size, tiles),
        in_specs=[
            head_at(0),
            kv_at(2 * q_blocks),
            kv_at(2 * q_blocks + k_blocks),
            head_at(q_blocks),
            pl.BlockSpec((rows, 1), lambda g, h, t: (t, 0)),
            pl.BlockSpec((1, length), lambda g, h, t: (0, 0)),
        ],
        out_specs=[
            pl.BlockSpec((rows, HEAD_WIDTH), lambda g, h, t: (t, g * group_size + h)),
            kv_at(0),
            kv_at(0),
        ],
        out_shape=[
            jax.ShapeDtypeStruct((length, q_width), jnp.bfloat16),
            jax.ShapeDtypeStruct((length, k_width), jnp.float32),
            jax.ShapeDtypeStruct((length, k_width), jnp.float32),
        ],
        compiler_params=pltpu.CompilerParams(
            dimension_semantics=("arbitrary", "arbitrary", "arbitrary"),
            vmem_limit_bytes=48 * 1024 * 1024,
        ),
    )(merged, merged, merged, merged, doc_ids.reshape(length, 1), doc_ids.reshape(1, length))
    return (query_out, key_acc.astype(jnp.bfloat16), value_acc.astype(jnp.bfloat16))


def weight_kernel(own_ref, mirror_ref, own_value_ref, mirror_value_ref, out_ref):
    contract_first = (((0,), (0,)), ((), ()))
    total = lax.dot_general(own_ref[...], own_value_ref[...], contract_first,
                            preferred_element_type=jnp.float32)
    total = total + lax.dot_general(mirror_ref[...], mirror_value_ref[...], contract_first,
                                    preferred_element_type=jnp.float32)
    out_ref[...] = total.astype(out_ref.dtype)


def weight_grads(own_rows, mirror_rows, own_values, mirror_values):
    positions, width = own_rows.shape
    cols = own_values.shape[1]
    tile = min(width, 4096)
    row_spec = pl.BlockSpec((positions, tile), lambda i: (0, i))
    value_spec = pl.BlockSpec((positions, cols), lambda i: (0, 0))
    return pl.pallas_call(
        weight_kernel,
        grid=(width // tile,),
        in_specs=[row_spec, row_spec, value_spec, value_spec],
        out_specs=pl.BlockSpec((tile, cols), lambda i: (i, 0)),
        out_shape=jax.ShapeDtypeStruct((width, cols), jnp.bfloat16),
        compiler_params=pltpu.CompilerParams(
            dimension_semantics=("arbitrary",), vmem_limit_bytes=48 * 1024 * 1024
        ),
    )(own_rows, mirror_rows, own_values, mirror_values)


def local(queries, key_states, section_value_states, out_grad, layer_input, doc_segments):
    section_count = lax.axis_size("section")
    seq_count = lax.axis_size("seq")
    seq_index = lax.axis_index("seq")
    mirror = [(i, section_count - 1 - i) for i in range(section_count)]
    own_rows = layer_input[0]
    own_gathered = lax.all_gather(own_rows, "seq", axis=0, tiled=True)
    mirror_rows = lax.ppermute(own_rows, "section", mirror)
    positions = queries.shape[1]
    q_width = queries.shape[2] // seq_count
    k_width = key_states.shape[2] // seq_count
    parts = [
        queries[0].reshape(positions, seq_count, q_width),
        out_grad[0].reshape(positions, seq_count, q_width),
        key_states[0].reshape(positions, seq_count, k_width),
        section_value_states[0].reshape(positions, seq_count, k_width),
    ]
    merged = lax.all_to_all(
        jnp.concatenate(parts, axis=2), "seq", split_axis=1, concat_axis=0, tiled=True
    ).reshape(positions * seq_count, 2 * q_width + 2 * k_width)
    doc_ids = lax.all_to_all(
        jnp.broadcast_to(doc_segments, (seq_count, positions)), "seq",
        split_axis=0, concat_axis=0, tiled=True,
    ).reshape(seq_count * positions)
    merged, mirror_rows = lax.optimization_barrier((merged, mirror_rows))
    mirror_gathered = lax.all_gather(mirror_rows, "seq", axis=0, tiled=True)
    query_out, key_out, value_out = attention_grads(merged, doc_ids, q_width, k_width)
    back = lax.all_to_all(
        jnp.concatenate([query_out, key_out], axis=1), "seq", split_axis=0, concat_axis=0,
        tiled=True,
    ).reshape(seq_count, positions, q_width + k_width)
    query_back = jnp.concatenate([back[j, :, :q_width] for j in range(seq_count)], axis=1)
    key_back = jnp.concatenate([back[j, :, q_width:] for j in range(seq_count)], axis=1)
    mirror_value = lax.ppermute(value_out, "section", mirror)
    paired = weight_grads(own_gathered, mirror_gathered, value_out, mirror_value)
    return (query_back[None], key_back[None], paired[None])


def solution(mesh):
    in_specs = (
        P("section", "seq", None),
        P("section", "seq", None),
        P("section", "seq", None),
        P("section", "seq", None),
        P("section", "seq", None),
        P("section", "seq"),
    )
    out_specs = (P("section", "seq", None), P("section", "seq", None), P("section", None, "seq"))
    return jax.shard_map(local, mesh=mesh, in_specs=in_specs, out_specs=out_specs, check_vma=False)
```

```python
import math

import jax
import jax.numpy as jnp
from jax import lax
from jax.experimental import pallas as pl
from jax.experimental.pallas import tpu as pltpu
from jax.sharding import PartitionSpec as P

HEAD_WIDTH = 128


def attention_kernel(query_ref, key_ref, value_ref, grad_ref, doc_col_ref, doc_row_ref,
                     query_out_ref, key_out_ref, value_out_ref):
    head, tile = pl.program_id(1), pl.program_id(2)
    rows, length = query_ref.shape[0], key_ref.shape[0]
    scale_factor = 1.0 / math.sqrt(key_ref.shape[1])

    @pl.when((head == 0) & (tile == 0))
    def _():
        key_out_ref[...] = jnp.zeros(key_out_ref.shape, jnp.float32)
        value_out_ref[...] = jnp.zeros(value_out_ref.shape, jnp.float32)

    query_one, grad_one = query_ref[...], grad_ref[...]
    key_col, value_col = key_ref[...], value_ref[...]
    row_pos = tile * rows + lax.broadcasted_iota(jnp.int32, (rows, length), 0)
    col_pos = lax.broadcasted_iota(jnp.int32, (rows, length), 1)
    allowed = (row_pos >= col_pos) & (doc_col_ref[...] == doc_row_ref[...])
    contract_last = (((1,), (1,)), ((), ()))
    contract_first = (((0,), (0,)), ((), ()))
    scores = lax.dot_general(query_one, key_col, contract_last,
                             preferred_element_type=jnp.float32) * scale_factor
    scores = jnp.where(allowed, scores, -jnp.inf)
    row_max = jnp.max(scores, axis=1, keepdims=True)
    weights = jnp.exp(scores - row_max)
    attention = weights / jnp.sum(weights, axis=1, keepdims=True)
    probs_low = attention.astype(jnp.bfloat16)
    attended = jnp.dot(probs_low, value_col, preferred_element_type=jnp.float32).astype(jnp.bfloat16)
    row_delta = jnp.sum(grad_one.astype(jnp.float32) * attended.astype(jnp.float32),
                        axis=1, keepdims=True)
    dprobs = lax.dot_general(grad_one, value_col, contract_last,
                             preferred_element_type=jnp.float32)
    dscores = (attention * (dprobs - row_delta) * scale_factor).astype(jnp.bfloat16)
    query_out_ref[...] = jnp.dot(dscores, key_col,
                                 preferred_element_type=jnp.float32).astype(jnp.bfloat16)
    key_out_ref[...] += lax.dot_general(dscores, query_one, contract_first,
                                        preferred_element_type=jnp.float32)
    value_out_ref[...] += lax.dot_general(probs_low, grad_one, contract_first,
                                          preferred_element_type=jnp.float32)


def attention_grads(merged, doc_ids, q_width, k_width):
    length = merged.shape[0]
    kv_heads = k_width // HEAD_WIDTH
    group_size = q_width // k_width
    rows = min(length, 256)
    tiles = length // rows
    q_blocks, k_blocks = q_width // HEAD_WIDTH, k_width // HEAD_WIDTH

    def head_at(base):
        return pl.BlockSpec((rows, HEAD_WIDTH), lambda g, h, t: (t, base + g * group_size + h))

    def kv_at(base):
        return pl.BlockSpec((length, HEAD_WIDTH), lambda g, h, t: (0, base + g))

    query_out, key_acc, value_acc = pl.pallas_call(
        attention_kernel,
        grid=(kv_heads, group_size, tiles),
        in_specs=[
            head_at(0),
            kv_at(2 * q_blocks),
            kv_at(2 * q_blocks + k_blocks),
            head_at(q_blocks),
            pl.BlockSpec((rows, 1), lambda g, h, t: (t, 0)),
            pl.BlockSpec((1, length), lambda g, h, t: (0, 0)),
        ],
        out_specs=[
            pl.BlockSpec((rows, HEAD_WIDTH), lambda g, h, t: (t, g * group_size + h)),
            kv_at(0),
            kv_at(0),
        ],
        out_shape=[
            jax.ShapeDtypeStruct((length, q_width), jnp.bfloat16),
            jax.ShapeDtypeStruct((length, k_width), jnp.float32),
            jax.ShapeDtypeStruct((length, k_width), jnp.float32),
        ],
        compiler_params=pltpu.CompilerParams(
            dimension_semantics=("arbitrary", "arbitrary", "arbitrary"),
            vmem_limit_bytes=48 * 1024 * 1024,
        ),
    )(merged, merged, merged, merged, doc_ids.reshape(length, 1), doc_ids.reshape(1, length))
    return (query_out, key_acc.astype(jnp.bfloat16), value_acc.astype(jnp.bfloat16))


def weight_kernel(own_ref, mirror_ref, own_value_ref, mirror_value_ref, out_ref):
    contract_first = (((0,), (0,)), ((), ()))
    total = lax.dot_general(own_ref[...], own_value_ref[...], contract_first,
                            preferred_element_type=jnp.float32)
    total = total + lax.dot_general(mirror_ref[...], mirror_value_ref[...], contract_first,
                                    preferred_element_type=jnp.float32)
    out_ref[...] = total.astype(out_ref.dtype)


def weight_grads(own_rows, mirror_rows, own_values, mirror_values):
    positions, width = own_rows.shape
    cols = own_values.shape[1]
    tile = min(width, 2048)
    while width % tile:
        tile //= 2
    row_spec = pl.BlockSpec((positions, tile), lambda i: (0, i))
    value_spec = pl.BlockSpec((positions, cols), lambda i: (0, 0))
    return pl.pallas_call(
        weight_kernel,
        grid=(width // tile,),
        in_specs=[row_spec, row_spec, value_spec, value_spec],
        out_specs=pl.BlockSpec((tile, cols), lambda i: (i, 0)),
        out_shape=jax.ShapeDtypeStruct((width, cols), jnp.bfloat16),
        compiler_params=pltpu.CompilerParams(
            dimension_semantics=("arbitrary",), vmem_limit_bytes=48 * 1024 * 1024
        ),
    )(own_rows, mirror_rows, own_values, mirror_values)


def local(queries, key_states, section_value_states, out_grad, layer_input, doc_segments):
    section_count = lax.axis_size("section")
    seq_count = lax.axis_size("seq")
    seq_index = lax.axis_index("seq")
    mirror = [(i, section_count - 1 - i) for i in range(section_count)]
    section_index = lax.axis_index("section")
    lower = section_index < section_count // 2
    width = layer_input.shape[2]
    span = width - width // 8
    rest = width - span
    own_start = jnp.where(lower, 0, rest)
    other_start = jnp.where(lower, rest, 0)
    own_half = lax.dynamic_slice_in_dim(layer_input[0], own_start, span, axis=1)
    other_half = lax.dynamic_slice_in_dim(layer_input[0], other_start, span, axis=1)
    own_gathered = lax.all_gather(own_half, "seq", axis=0, tiled=True)
    mirror_rows = lax.ppermute(other_half, "section", mirror)
    positions = queries.shape[1]
    q_width = queries.shape[2] // seq_count
    k_width = key_states.shape[2] // seq_count
    parts = [
        queries[0].reshape(positions, seq_count, q_width),
        out_grad[0].reshape(positions, seq_count, q_width),
        key_states[0].reshape(positions, seq_count, k_width),
        section_value_states[0].reshape(positions, seq_count, k_width),
    ]
    merged = lax.all_to_all(
        jnp.concatenate(parts, axis=2), "seq", split_axis=1, concat_axis=0, tiled=True
    ).reshape(positions * seq_count, 2 * q_width + 2 * k_width)
    doc_ids = lax.all_to_all(
        jnp.broadcast_to(doc_segments, (seq_count, positions)), "seq",
        split_axis=0, concat_axis=0, tiled=True,
    ).reshape(seq_count * positions)
    merged, mirror_rows = lax.optimization_barrier((merged, mirror_rows))
    mirror_gathered = lax.all_gather(mirror_rows, "seq", axis=0, tiled=True)
    query_out, key_out, value_out = attention_grads(merged, doc_ids, q_width, k_width)
    back = lax.all_to_all(
        jnp.concatenate([query_out, key_out], axis=1), "seq", split_axis=0, concat_axis=0,
        tiled=True,
    ).reshape(seq_count, positions, q_width + k_width)
    query_back = jnp.concatenate([back[j, :, :q_width] for j in range(seq_count)], axis=1)
    key_back = jnp.concatenate([back[j, :, q_width:] for j in range(seq_count)], axis=1)
    mirror_value = lax.ppermute(value_out, "section", mirror)
    mine = weight_grads(own_gathered, mirror_gathered, value_out, mirror_value)
    shared = lax.dynamic_slice_in_dim(mine, jnp.where(lower, 0, span - rest), rest, axis=0)
    theirs = lax.ppermute(shared, "section", mirror)
    paired = jnp.where(
        lower,
        jnp.concatenate([mine, theirs], axis=0),
        jnp.concatenate([theirs, mine], axis=0),
    )
    return (query_back[None], key_back[None], paired[None])


def solution(mesh):
    in_specs = (
        P("section", "seq", None),
        P("section", "seq", None),
        P("section", "seq", None),
        P("section", "seq", None),
        P("section", "seq", None),
        P("section", "seq"),
    )
    out_specs = (P("section", "seq", None), P("section", "seq", None), P("section", None, "seq"))
    return jax.shard_map(local, mesh=mesh, in_specs=in_specs, out_specs=out_specs, check_vma=False)
```

```python
import math

import jax
import jax.numpy as jnp
from jax import lax
from jax.experimental import pallas as pl
from jax.experimental.pallas import tpu as pltpu
from jax.sharding import PartitionSpec as P

HEAD_WIDTH = 128


def attention_kernel(query_ref, key_ref, value_ref, grad_ref, doc_col_ref, doc_row_ref,
                     query_out_ref, key_out_ref, value_out_ref):
    head, tile = pl.program_id(1), pl.program_id(2)
    rows, length = query_ref.shape[0], key_ref.shape[0]
    scale_factor = 1.0 / math.sqrt(key_ref.shape[1])

    @pl.when((head == 0) & (tile == 0))
    def _():
        key_out_ref[...] = jnp.zeros(key_out_ref.shape, jnp.float32)
        value_out_ref[...] = jnp.zeros(value_out_ref.shape, jnp.float32)

    query_one, grad_one = query_ref[...], grad_ref[...]
    key_col, value_col = key_ref[...], value_ref[...]
    row_pos = tile * rows + lax.broadcasted_iota(jnp.int32, (rows, length), 0)
    col_pos = lax.broadcasted_iota(jnp.int32, (rows, length), 1)
    allowed = (row_pos >= col_pos) & (doc_col_ref[...] == doc_row_ref[...])
    contract_last = (((1,), (1,)), ((), ()))
    contract_first = (((0,), (0,)), ((), ()))
    scores = lax.dot_general(query_one, key_col, contract_last,
                             preferred_element_type=jnp.float32) * scale_factor
    scores = jnp.where(allowed, scores, -jnp.inf)
    row_max = jnp.max(scores, axis=1, keepdims=True)
    weights = jnp.exp(scores - row_max)
    attention = weights / jnp.sum(weights, axis=1, keepdims=True)
    probs_low = attention.astype(jnp.bfloat16)
    attended = jnp.dot(probs_low, value_col, preferred_element_type=jnp.float32).astype(jnp.bfloat16)
    row_delta = jnp.sum(grad_one.astype(jnp.float32) * attended.astype(jnp.float32),
                        axis=1, keepdims=True)
    dprobs = lax.dot_general(grad_one, value_col, contract_last,
                             preferred_element_type=jnp.float32)
    dscores = (attention * (dprobs - row_delta) * scale_factor).astype(jnp.bfloat16)
    query_out_ref[...] = jnp.dot(dscores, key_col,
                                 preferred_element_type=jnp.float32).astype(jnp.bfloat16)
    key_out_ref[...] += lax.dot_general(dscores, query_one, contract_first,
                                        preferred_element_type=jnp.float32)
    value_out_ref[...] += lax.dot_general(probs_low, grad_one, contract_first,
                                          preferred_element_type=jnp.float32)


def attention_grads(merged, doc_ids, q_width, k_width):
    length = merged.shape[0]
    kv_heads = k_width // HEAD_WIDTH
    group_size = q_width // k_width
    rows = min(length, 256)
    tiles = length // rows
    q_blocks, k_blocks = q_width // HEAD_WIDTH, k_width // HEAD_WIDTH

    def head_at(base):
        return pl.BlockSpec((rows, HEAD_WIDTH), lambda g, h, t: (t, base + g * group_size + h))

    def kv_at(base):
        return pl.BlockSpec((length, HEAD_WIDTH), lambda g, h, t: (0, base + g))

    query_out, key_acc, value_acc = pl.pallas_call(
        attention_kernel,
        grid=(kv_heads, group_size, tiles),
        in_specs=[
            head_at(0),
            kv_at(2 * q_blocks),
            kv_at(2 * q_blocks + k_blocks),
            head_at(q_blocks),
            pl.BlockSpec((rows, 1), lambda g, h, t: (t, 0)),
            pl.BlockSpec((1, length), lambda g, h, t: (0, 0)),
        ],
        out_specs=[
            pl.BlockSpec((rows, HEAD_WIDTH), lambda g, h, t: (t, g * group_size + h)),
            kv_at(0),
            kv_at(0),
        ],
        out_shape=[
            jax.ShapeDtypeStruct((length, q_width), jnp.bfloat16),
            jax.ShapeDtypeStruct((length, k_width), jnp.float32),
            jax.ShapeDtypeStruct((length, k_width), jnp.float32),
        ],
        compiler_params=pltpu.CompilerParams(
            dimension_semantics=("arbitrary", "arbitrary", "arbitrary"),
            vmem_limit_bytes=48 * 1024 * 1024,
        ),
    )(merged, merged, merged, merged, doc_ids.reshape(length, 1), doc_ids.reshape(1, length))
    return (query_out, key_acc.astype(jnp.bfloat16), value_acc.astype(jnp.bfloat16))


def weight_kernel(own_ref, mirror_ref, own_value_ref, mirror_value_ref, out_ref):
    contract_first = (((0,), (0,)), ((), ()))
    total = lax.dot_general(own_ref[...], own_value_ref[...], contract_first,
                            preferred_element_type=jnp.float32)
    total = total + lax.dot_general(mirror_ref[...], mirror_value_ref[...], contract_first,
                                    preferred_element_type=jnp.float32)
    out_ref[...] = total.astype(out_ref.dtype)


def weight_grads(own_rows, mirror_rows, own_values, mirror_values):
    positions, width = own_rows.shape
    cols = own_values.shape[1]
    tile = min(width, 4096)
    row_spec = pl.BlockSpec((positions, tile), lambda i: (0, i))
    value_spec = pl.BlockSpec((positions, cols), lambda i: (0, 0))
    return pl.pallas_call(
        weight_kernel,
        grid=(width // tile,),
        in_specs=[row_spec, row_spec, value_spec, value_spec],
        out_specs=pl.BlockSpec((tile, cols), lambda i: (i, 0)),
        out_shape=jax.ShapeDtypeStruct((width, cols), jnp.bfloat16),
        compiler_params=pltpu.CompilerParams(
            dimension_semantics=("arbitrary",), vmem_limit_bytes=48 * 1024 * 1024
        ),
    )(own_rows, mirror_rows, own_values, mirror_values)


def seq_gather(rows, count):
    if count != 4:
        return lax.all_gather(rows, "seq", axis=0, tiled=True)
    pairs = lax.all_gather(rows, "seq", axis=0, tiled=True, axis_index_groups=[[0, 1], [2, 3]])
    return lax.all_gather(pairs, "seq", axis=0, tiled=True, axis_index_groups=[[0, 2], [1, 3]])


def local(queries, key_states, section_value_states, out_grad, layer_input, doc_segments):
    section_count = lax.axis_size("section")
    seq_count = lax.axis_size("seq")
    seq_index = lax.axis_index("seq")
    mirror = [(i, section_count - 1 - i) for i in range(section_count)]
    own_rows = layer_input[0]
    own_gathered = seq_gather(own_rows, seq_count)
    mirror_rows = lax.ppermute(own_rows, "section", mirror)
    positions = queries.shape[1]
    q_width = queries.shape[2] // seq_count
    k_width = key_states.shape[2] // seq_count
    parts = [
        queries[0].reshape(positions, seq_count, q_width),
        out_grad[0].reshape(positions, seq_count, q_width),
        key_states[0].reshape(positions, seq_count, k_width),
        section_value_states[0].reshape(positions, seq_count, k_width),
    ]
    merged = lax.all_to_all(
        jnp.concatenate(parts, axis=2), "seq", split_axis=1, concat_axis=0, tiled=True
    ).reshape(positions * seq_count, 2 * q_width + 2 * k_width)
    doc_ids = lax.all_to_all(
        jnp.broadcast_to(doc_segments, (seq_count, positions)), "seq",
        split_axis=0, concat_axis=0, tiled=True,
    ).reshape(seq_count * positions)
    merged, mirror_rows = lax.optimization_barrier((merged, mirror_rows))
    mirror_gathered = seq_gather(mirror_rows, seq_count)
    query_out, key_out, value_out = attention_grads(merged, doc_ids, q_width, k_width)
    back = lax.all_to_all(
        jnp.concatenate([query_out, key_out], axis=1), "seq", split_axis=0, concat_axis=0,
        tiled=True,
    ).reshape(seq_count, positions, q_width + k_width)
    query_back = jnp.concatenate([back[j, :, :q_width] for j in range(seq_count)], axis=1)
    key_back = jnp.concatenate([back[j, :, q_width:] for j in range(seq_count)], axis=1)
    mirror_value = lax.ppermute(value_out, "section", mirror)
    paired = weight_grads(own_gathered, mirror_gathered, value_out, mirror_value)
    return (query_back[None], key_back[None], paired[None])


def solution(mesh):
    in_specs = (
        P("section", "seq", None),
        P("section", "seq", None),
        P("section", "seq", None),
        P("section", "seq", None),
        P("section", "seq", None),
        P("section", "seq"),
    )
    out_specs = (P("section", "seq", None), P("section", "seq", None), P("section", None, "seq"))
    return jax.shard_map(local, mesh=mesh, in_specs=in_specs, out_specs=out_specs, check_vma=False)
```
